32 devices in a mesh: ctx: 8 (over z, x), probe: 4 (over y, core).
Axes of the slice: x: 2, y: 2, z: 4, core: 2. Of those that a mesh axis runs over, the one named last changes fastest.
Arguments:
- features: float32 [3, 2048, 1024], P(None, 'ctx'), may hold values from -6 to 6
- cotangent: float32 [2048, 1024], P('ctx'), may hold values from -48 to 48
- gate_logits: float32 [4], replicated, may hold values from -4 to 4
- probes: int32 [4, 3, 2048, 1024], P('probe', None, 'ctx'), may hold values from -1 to 1, as said below
Outputs:
- products: float32 [4, 3, 2048, 1024], P('probe', None, 'ctx')
- block_trace: float32 [8, 3, 4], P('ctx')
The draws below stay inside these ranges and needn't reach their ends.
Inputs may be any that keep to these rules, and one draw needn't show every extreme that they name: `probes`: every entry is -1 or 1.
All inputs are finite; a program needn't handle non-finite values.
Results may differ from the reference program's by a relative error of at most 0.0003.
Values sent between devices are 32-bit elements; how exact they have to be, the bound alone decides.
No kernel may reach another device: no remote copies, remote signals or barrier semaphores. Data moves between devices by JAX's collectives and lax.ppermute only.
A program may use at most 192 MiB of HBM per device.

```python
import jax
import jax.numpy as jnp
from jax import lax

H = 4
DH = 256
SEG = 256
PROBES = 4
TOKENS = 2048
N_CTX = 8


def draw_probes(key, part):
    coin_flips = jax.random.randint(key, (PROBES, 3, TOKENS, H * DH), 0, 2)
    return (2 * coin_flips - 1).astype(jnp.int32)


def steps_of(rng, extent, cuts, low, largest):
    factor_of, own = 1.0, jax.random.fold_in(rng, 6)
    for position, shards_of in cuts:
        draws = jnp.exp(jax.random.uniform(jax.random.fold_in(own, position), (shards_of,), jnp.float32, low / len(cuts), largest / len(cuts)))
        factor_of = factor_of * jnp.repeat(draws, extent[position] // shards_of).reshape([-1 if axis == position else 1 for axis in range(len(extent))])
    return factor_of


def bell_draw(key, extent, scale, bound, cuts=(), dtype=jnp.bfloat16):
    result = jax.random.normal(key, extent, jnp.float32) * scale
    if len(cuts) > 0:
        result = steps_of(key, extent, cuts, -0.22, 0.18) * result
    return jnp.clip(result, min=-bound, max=bound).astype(dtype)


def setup_inputs(seed: int = 0) -> dict:
    splits = jax.random.split(jax.random.key(seed), 5)
    features = bell_draw(splits[0], (3, TOKENS, H * DH), 1.0, 6.0, ((1, 8),), jnp.float32)
    cotangent = bell_draw(splits[1], (TOKENS, H * DH), 8.0, 48.0, ((0, 8),), jnp.float32)
    gate_logits = bell_draw(splits[2], (H,), 1.5, 4.0, (), jnp.float32)
    probes = draw_probes(jax.random.fold_in(splits[4], 71), 0)
    return {"features": features, "cotangent": cotangent, "gate_logits": gate_logits, "probes": probes}


HIGHEST = lax.Precision.HIGHEST

def feature_map(inputs):
    return jnp.where(inputs > 0, inputs + 1.0, jnp.exp(jnp.minimum(inputs, 0.0)))

def segment_loss(query_rows, key_rows, value_rows, memory, normalizer, cot_rows, gate_logits):
    query_feat = feature_map(query_rows)
    retrieved = jnp.einsum('sha,hab->shb', query_feat, memory, precision=HIGHEST)
    denom_mem = jnp.einsum('sha,ha->sh', query_feat, normalizer, precision=HIGHEST) + 1.0
    from_memory = retrieved / denom_mem[:, :, None]
    seg_rows = query_rows.shape[0]
    scale = query_rows.shape[-1] ** (-0.5)
    causal = lax.broadcasted_iota(jnp.int32, (seg_rows, seg_rows), 0) >= lax.broadcasted_iota(jnp.int32, (seg_rows, seg_rows), 1)
    logits = jnp.einsum('sha,tha->hst', query_rows, key_rows, precision=HIGHEST) * scale
    logits = jnp.where(causal[None], logits, -1e+30)
    top = lax.stop_gradient(lax.optimization_barrier(jnp.max(logits, axis=2, keepdims=True)))
    weights = jnp.exp(logits - top)
    local_num = jnp.einsum('hst,thb->shb', weights, value_rows, precision=HIGHEST)
    local_den = jnp.transpose(lax.optimization_barrier(jnp.sum(weights, axis=2)))
    from_local = local_num / local_den[:, :, None]
    mixing = jax.nn.sigmoid(gate_logits)[None, :, None]
    output = mixing * from_memory + (1.0 - mixing) * from_local
    return jnp.sum(cot_rows * output)

def total_loss(features, cotangent, gate_logits):
    shaped = features.reshape(3, N_CTX, SEG, H, DH)
    cot_shaped = cotangent.reshape(N_CTX, SEG, H, DH)

    def advance(carried, pieces):
        memory, normalizer, running = carried
        query_rows, key_rows, value_rows, cot_rows = pieces
        running = running + segment_loss(query_rows, key_rows, value_rows, memory, normalizer, cot_rows, gate_logits)
        key_feat = feature_map(key_rows)
        memory = memory + jnp.einsum('sha,shb->hab', key_feat, value_rows, precision=HIGHEST)
        normalizer = normalizer + lax.optimization_barrier(jnp.sum(key_feat, axis=0))
        return ((memory, normalizer, running), None)
    initial = (jnp.zeros((H, DH, DH), jnp.float32), jnp.zeros((H, DH), jnp.float32), jnp.zeros((), jnp.float32))
    finished, _ = lax.scan(advance, initial, (shaped[0], shaped[1], shaped[2], cot_shaped))
    return finished[2]

def reference(features, cotangent, gate_logits, probes):
    gradient = jax.grad(total_loss)
    results = []
    for probe_index in range(PROBES):
        direction = probes[probe_index].astype(jnp.float32)

        def directional(features_at):
            return jnp.sum(gradient(features_at, cotangent, gate_logits) * direction)
        results.append(jax.grad(directional)(features))
    products = jnp.stack(results)
    weighted = (probes.astype(jnp.float32) * products).reshape(PROBES, 3, N_CTX, SEG, H, DH)
    block_trace = jnp.transpose(lax.optimization_barrier(jnp.sum(weighted, axis=(0, 3, 5))), (1, 0, 2)) / (SEG * PROBES)
    return (products, block_trace)
```

```python
import jax
import jax.numpy as jnp
from jax import lax
from jax.sharding import PartitionSpec as P

HIGH = lax.Precision.HIGH


def exclusive(block, reverse):
    zero = jnp.zeros_like(block[:1])
    if reverse:
        later = jnp.flip(jnp.cumsum(jnp.flip(block[1:], 0), axis=0), 0)
        return jnp.concatenate((later, zero), axis=0)
    return jnp.concatenate((zero, jnp.cumsum(block[:-1], axis=0)), axis=0)


def packed_scan(groups_of_parts, axis):
    count = lax.axis_size(axis)
    width = groups_of_parts[0][0][0].shape[-1]
    blocks, layout = [], []
    for parts, reverse in groups_of_parts:
        rows = [p.reshape(-1, width) for p in parts]
        sizes = [r.shape[0] for r in rows]
        total = sum(sizes)
        unit = 8 * count
        padded = -(-total // unit) * unit
        if padded > total:
            rows.append(jnp.zeros((padded - total, width), jnp.float32))
        blocks.append(jnp.concatenate(rows, axis=0).reshape(count, padded // count, width))
        layout.append((parts, sizes, padded, reverse))
    buffer = jnp.concatenate(blocks, axis=1) if len(blocks) > 1 else blocks[0]
    spread = lax.all_to_all(buffer, axis, 0, 0)
    scanned, offset = [], 0
    for parts, sizes, padded, reverse in layout:
        chunk = padded // count
        scanned.append(exclusive(spread[:, offset:offset + chunk], reverse))
        offset += chunk
    scanned = jnp.concatenate(scanned, axis=1) if len(scanned) > 1 else scanned[0]
    back = lax.all_to_all(scanned, axis, 0, 0)
    outs, offset = [], 0
    for parts, sizes, padded, reverse in layout:
        chunk = padded // count
        flat = back[:, offset:offset + chunk].reshape(padded, width)
        offset += chunk
        row = 0
        mine = []
        for p, size in zip(parts, sizes):
            mine.append(flat[row:row + size].reshape(p.shape))
            row += size
        outs.append(mine)
    return outs


def feature_map(inputs):
    return jnp.where(inputs > 0, inputs + 1.0, jnp.exp(jnp.minimum(inputs, 0.0)))


def feature_slope(inputs):
    return jnp.where(inputs > 0, 1.0, jnp.exp(jnp.minimum(inputs, 0.0)))


def feature_curve(inputs):
    return jnp.where(inputs > 0, 0.0, jnp.exp(jnp.minimum(inputs, 0.0)))


def local_loss(query_rows, key_rows, value_rows, weight_rows):
    seg_rows = query_rows.shape[0]
    scale = query_rows.shape[-1] ** (-0.5)
    causal = lax.broadcasted_iota(jnp.int32, (seg_rows, seg_rows), 0) >= lax.broadcasted_iota(
        jnp.int32, (seg_rows, seg_rows), 1
    )
    logits = jnp.einsum("sha,tha->hst", query_rows, key_rows, precision=HIGH) * scale
    logits = jnp.where(causal[None], logits, -1e30)
    top = lax.stop_gradient(jnp.max(logits, axis=2, keepdims=True))
    weights = jnp.exp(logits - top)
    local_num = jnp.einsum("hst,thb->shb", weights, value_rows, precision=HIGH)
    local_den = jnp.transpose(jnp.sum(weights, axis=2))
    from_local = local_num / local_den[:, :, None]
    return jnp.sum(weight_rows * from_local)


def memory_loss(query_rows, memory, normalizer, weight_rows):
    query_feat = feature_map(query_rows)
    retrieved = jnp.einsum("sha,hab->shb", query_feat, memory, precision=HIGH)
    denom_mem = jnp.einsum("sha,ha->sh", query_feat, normalizer, precision=HIGH) + 1.0
    return jnp.sum(weight_rows * retrieved / denom_mem[:, :, None])


def memory_slope(query_rows, normalizer, weight_rows):
    query_feat = feature_map(query_rows)
    denom_mem = jnp.einsum("sha,ha->sh", query_feat, normalizer, precision=HIGH) + 1.0
    return jnp.einsum("sha,shb->hab", query_feat, weight_rows / denom_mem[:, :, None], precision=HIGH)


def shards(features, cotangent, gate_logits, probes):
    heads = gate_logits.shape[0]
    seg_rows = features.shape[1]
    head_size = features.shape[2] // heads
    shaped = features.reshape(3, seg_rows, heads, head_size)
    query_rows, key_rows, value_rows = (shaped[0], shaped[1], shaped[2])
    cot_rows = cotangent.reshape(seg_rows, heads, head_size)
    mixing = jax.nn.sigmoid(gate_logits)[None, :, None]
    mem_weight = cot_rows * mixing
    loc_weight = cot_rows * (1.0 - mixing)
    signs = probes[0].astype(jnp.float32).reshape(3, seg_rows, heads, head_size)
    query_dir, key_dir, value_dir = (signs[0], signs[1], signs[2])
    key_feat = feature_map(key_rows)
    key_slope = feature_slope(key_rows)
    key_tan = key_slope * key_dir
    groups = lax.axis_size("probe")
    share = heads // groups
    first_head = lax.axis_index("probe") * share

    norm_inc = jnp.sum(key_feat, axis=0)
    norm_tan = jnp.sum(key_tan, axis=0)
    ((normalizer, normalizer_tan),) = packed_scan([((norm_inc, norm_tan), False)], "ctx")

    increment = jnp.einsum("sha,shb->hab", key_feat, value_rows, precision=HIGH)
    increment_tan = jnp.einsum("sha,shb->hab", key_tan, value_rows, precision=HIGH) + jnp.einsum(
        "sha,shb->hab", key_feat, value_dir, precision=HIGH
    )
    slope, slope_tan = jax.jvp(
        lambda q, n: memory_slope(q, n, mem_weight), (query_rows, normalizer), (query_dir, normalizer_tan)
    )
    own_inc = lax.dynamic_slice_in_dim(increment, first_head, share, 0)
    own_slope = lax.dynamic_slice_in_dim(slope, first_head, share, 0)
    (own_prefix, memory_tan), (own_suffix, back_mem_tan) = packed_scan(
        [((own_inc, increment_tan), False), ((own_slope, slope_tan), True)], "ctx"
    )

    local_grad = jax.grad(local_loss, argnums=(0, 1, 2))
    _, local_curv = jax.jvp(
        lambda q, k, v: local_grad(q, k, v, loc_weight),
        (query_rows, key_rows, value_rows),
        (query_dir, key_dir, value_dir),
    )

    both = lax.all_gather(jnp.stack((own_prefix, own_suffix)), "probe", axis=1, tiled=True)
    memory, back_mem = both[0], both[1]

    mem_grad = jax.grad(memory_loss, argnums=(0, 2))
    (_, back_norm_inc), (query_curv, back_norm_inc_tan) = jax.jvp(
        lambda q, m, n: mem_grad(q, m, n, mem_weight),
        (query_rows, memory, normalizer),
        (query_dir, memory_tan, normalizer_tan),
    )
    ((back_norm, back_norm_tan),) = packed_scan([((back_norm_inc, back_norm_inc_tan), True)], "ctx")

    through = jnp.einsum("shb,hab->sha", value_rows, back_mem, precision=HIGH) + back_norm[None]
    through_tan = (
        jnp.einsum("shb,hab->sha", value_dir, back_mem, precision=HIGH)
        + jnp.einsum("shb,hab->sha", value_rows, back_mem_tan, precision=HIGH)
        + back_norm_tan[None]
    )
    query_out = local_curv[0] + query_curv
    key_out = local_curv[1] + feature_curve(key_rows) * key_dir * through + key_slope * through_tan
    value_out = (
        local_curv[2]
        + jnp.einsum("sha,hab->shb", key_tan, back_mem, precision=HIGH)
        + jnp.einsum("sha,hab->shb", key_feat, back_mem_tan, precision=HIGH)
    )
    stacked = jnp.stack((query_out, key_out, value_out))
    products = stacked.reshape(1, 3, seg_rows, heads * head_size)
    partial_trace = jnp.sum(signs * stacked, axis=(1, 3)) / (seg_rows * groups)
    block_trace = lax.psum(partial_trace, "probe")
    return (products, block_trace.reshape(1, 3, heads))


def solution(mesh):
    placed = (P(None, "ctx", None), P("ctx", None), P(), P("probe", None, "ctx", None))
    return jax.shard_map(
        shards,
        mesh=mesh,
        in_specs=placed,
        out_specs=(P("probe", None, "ctx", None), P("ctx", None, None)),
        check_vma=False,
    )
```

```python
import jax
import jax.numpy as jnp
from jax import lax
from jax.sharding import PartitionSpec as P

HIGH = lax.Precision.HIGH


def exclusive(block, reverse):
    count = block.shape[0]
    here = lax.broadcasted_iota(jnp.int32, (count, count), 0)
    there = lax.broadcasted_iota(jnp.int32, (count, count), 1)
    mask = (there > here) if reverse else (there < here)
    flat = block.reshape(count, -1)
    summed = jnp.dot(mask.astype(jnp.float32), flat, precision=lax.Precision.HIGHEST)
    return summed.reshape(block.shape)


def packed_scan(parts, axis, reverse):
    count = lax.axis_size(axis)
    width = parts[0].shape[-1]
    rows = [p.reshape(-1, width) for p in parts]
    sizes = [r.shape[0] for r in rows]
    total = sum(sizes)
    unit = 8 * count
    padded = -(-total // unit) * unit
    if padded > total:
        rows.append(jnp.zeros((padded - total, width), jnp.float32))
    buffer = jnp.concatenate(rows, axis=0).reshape(count, padded // count, width)
    spread = lax.all_to_all(buffer, axis, 0, 0)
    back = lax.all_to_all(exclusive(spread, reverse), axis, 0, 0).reshape(padded, width)
    outs, row = [], 0
    for p, size in zip(parts, sizes):
        outs.append(back[row:row + size].reshape(p.shape))
        row += size
    return outs


def feature_map(inputs):
    return jnp.where(inputs > 0, inputs + 1.0, jnp.exp(jnp.minimum(inputs, 0.0)))


def feature_slope(inputs):
    return jnp.where(inputs > 0, 1.0, jnp.exp(jnp.minimum(inputs, 0.0)))


def feature_curve(inputs):
    return jnp.where(inputs > 0, 0.0, jnp.exp(jnp.minimum(inputs, 0.0)))


def local_loss(query_rows, key_rows, value_rows, weight_rows):
    seg_rows = query_rows.shape[0]
    scale = query_rows.shape[-1] ** (-0.5)
    causal = lax.broadcasted_iota(jnp.int32, (seg_rows, seg_rows), 0) >= lax.broadcasted_iota(
        jnp.int32, (seg_rows, seg_rows), 1
    )
    logits = jnp.einsum("sha,tha->hst", query_rows, key_rows, precision=HIGH) * scale
    logits = jnp.where(causal[None], logits, -1e30)
    top = lax.stop_gradient(jnp.max(logits, axis=2, keepdims=True))
    weights = jnp.exp(logits - top)
    local_num = jnp.einsum("hst,thb->shb", weights, value_rows, precision=HIGH)
    local_den = jnp.transpose(jnp.sum(weights, axis=2))
    from_local = local_num / local_den[:, :, None]
    return jnp.sum(weight_rows * from_local)


def memory_loss(query_rows, memory, normalizer, weight_rows):
    query_feat = feature_map(query_rows)
    retrieved = jnp.einsum("sha,hab->shb", query_feat, memory, precision=HIGH)
    denom_mem = jnp.einsum("sha,ha->sh", query_feat, normalizer, precision=HIGH) + 1.0
    return jnp.sum(weight_rows * retrieved / denom_mem[:, :, None])


def memory_slope(query_rows, normalizer, weight_rows):
    query_feat = feature_map(query_rows)
    denom_mem = jnp.einsum("sha,ha->sh", query_feat, normalizer, precision=HIGH) + 1.0
    return jnp.einsum("sha,shb->hab", query_feat, weight_rows / denom_mem[:, :, None], precision=HIGH)


def shards(features, cotangent, gate_logits, probes):
    heads = gate_logits.shape[0]
    seg_rows = features.shape[1]
    head_size = features.shape[2] // heads
    shaped = features.reshape(3, seg_rows, heads, head_size)
    query_rows, key_rows, value_rows = (shaped[0], shaped[1], shaped[2])
    cot_rows = cotangent.reshape(seg_rows, heads, head_size)
    mixing = jax.nn.sigmoid(gate_logits)[None, :, None]
    mem_weight = cot_rows * mixing
    loc_weight = cot_rows * (1.0 - mixing)
    signs = probes[0].astype(jnp.float32).reshape(3, seg_rows, heads, head_size)
    query_dir, key_dir, value_dir = (signs[0], signs[1], signs[2])
    key_feat = feature_map(key_rows)
    key_slope = feature_slope(key_rows)
    key_tan = key_slope * key_dir
    groups = lax.axis_size("probe")
    share = heads // groups
    first_head = lax.axis_index("probe") * share

    local_grad = jax.grad(local_loss, argnums=(0, 1, 2))
    _, local_curv = jax.jvp(
        lambda q, k, v: local_grad(q, k, v, loc_weight),
        (query_rows, key_rows, value_rows),
        (query_dir, key_dir, value_dir),
    )

    increment = jnp.einsum("sha,shb->hab", key_feat, value_rows, precision=HIGH)
    increment_tan = jnp.einsum("sha,shb->hab", key_tan, value_rows, precision=HIGH) + jnp.einsum(
        "sha,shb->hab", key_feat, value_dir, precision=HIGH
    )
    norm_inc = jnp.sum(key_feat, axis=0)
    norm_tan = jnp.sum(key_tan, axis=0)
    own_inc = lax.dynamic_slice_in_dim(increment, first_head, share, 0)
    own_prefix, memory_tan, norms = packed_scan(
        (own_inc, increment_tan, jnp.concatenate((norm_inc, norm_tan), axis=0)), "ctx", False
    )
    normalizer, normalizer_tan = norms[:heads], norms[heads:]
    memory = lax.all_gather(own_prefix, "probe", axis=0, tiled=True)

    slope, slope_tan = jax.jvp(
        lambda q, n: memory_slope(q, n, mem_weight), (query_rows, normalizer), (query_dir, normalizer_tan)
    )
    mem_grad = jax.grad(memory_loss, argnums=(0, 2))
    (_, back_norm_inc), (query_curv, back_norm_inc_tan) = jax.jvp(
        lambda q, m, n: mem_grad(q, m, n, mem_weight),
        (query_rows, memory, normalizer),
        (query_dir, memory_tan, normalizer_tan),
    )
    own_slope = lax.dynamic_slice_in_dim(slope, first_head, share, 0)
    own_suffix, back_mem_tan, back_norms = packed_scan(
        (own_slope, slope_tan, jnp.concatenate((back_norm_inc, back_norm_inc_tan), axis=0)), "ctx", True
    )
    back_norm, back_norm_tan = back_norms[:heads], back_norms[heads:]
    back_mem = lax.all_gather(own_suffix, "probe", axis=0, tiled=True)

    through = jnp.einsum("shb,hab->sha", value_rows, back_mem, precision=HIGH) + back_norm[None]
    through_tan = (
        jnp.einsum("shb,hab->sha", value_dir, back_mem, precision=HIGH)
        + jnp.einsum("shb,hab->sha", value_rows, back_mem_tan, precision=HIGH)
        + back_norm_tan[None]
    )
    query_out = local_curv[0] + query_curv
    key_out = local_curv[1] + feature_curve(key_rows) * key_dir * through + key_slope * through_tan
    value_out = (
        local_curv[2]
        + jnp.einsum("sha,hab->shb", key_tan, back_mem, precision=HIGH)
        + jnp.einsum("sha,hab->shb", key_feat, back_mem_tan, precision=HIGH)
    )
    stacked = jnp.stack((query_out, key_out, value_out))
    products = stacked.reshape(1, 3, seg_rows, heads * head_size)
    partial_trace = jnp.sum(signs * stacked, axis=(1, 3)) / (seg_rows * groups)
    block_trace = lax.psum(partial_trace, "probe")
    return (products, block_trace.reshape(1, 3, heads))


def solution(mesh):
    placed = (P(None, "ctx", None), P("ctx", None), P(), P("probe", None, "ctx", None))
    return jax.shard_map(
        shards,
        mesh=mesh,
        in_specs=placed,
        out_specs=(P("probe", None, "ctx", None), P("ctx", None, None)),
        check_vma=False,
    )
```

```python
import jax
import jax.numpy as jnp
from jax import lax
from jax.sharding import PartitionSpec as P

HIGH = lax.Precision.HIGH


def exclusive(block, reverse):
    count = block.shape[0]
    here = lax.broadcasted_iota(jnp.int32, (count, count), 0)
    there = lax.broadcasted_iota(jnp.int32, (count, count), 1)
    mask = (there > here) if reverse else (there < here)
    flat = block.reshape(count, -1)
    summed = jnp.dot(mask.astype(jnp.float32), flat, precision=lax.Precision.HIGHEST)
    return summed.reshape(block.shape)


def exchange(blocks, axis):
    count = lax.axis_size(axis)
    place = lax.axis_index(axis)
    got = [lax.dynamic_index_in_dim(blocks, place, 0, False)]
    for shift in range(1, count):
        send = lax.dynamic_index_in_dim(blocks, (place + shift) % count, 0, False)
        got.append(lax.ppermute(send, axis, [(i, (i + shift) % count) for i in range(count)]))
    by_shift = jnp.stack(got)
    flipped = jnp.roll(by_shift[::-1], 1, axis=0)
    return jnp.roll(flipped, place, axis=0)


def packed_scan(parts, axis, reverse):
    count = lax.axis_size(axis)
    width = parts[0].shape[-1]
    rows = [p.reshape(-1, width) for p in parts]
    sizes = [r.shape[0] for r in rows]
    total = sum(sizes)
    unit = 8 * count
    padded = -(-total // unit) * unit
    if padded > total:
        rows.append(jnp.zeros((padded - total, width), jnp.float32))
    buffer = jnp.concatenate(rows, axis=0).reshape(count, padded // count, width)
    spread = exchange(buffer, axis)
    back = exchange(exclusive(spread, reverse), axis).reshape(padded, width)
    outs, row = [], 0
    for p, size in zip(parts, sizes):
        outs.append(back[row:row + size].reshape(p.shape))
        row += size
    return outs


def feature_map(inputs):
    return jnp.where(inputs > 0, inputs + 1.0, jnp.exp(jnp.minimum(inputs, 0.0)))


def feature_slope(inputs):
    return jnp.where(inputs > 0, 1.0, jnp.exp(jnp.minimum(inputs, 0.0)))


def feature_curve(inputs):
    return jnp.where(inputs > 0, 0.0, jnp.exp(jnp.minimum(inputs, 0.0)))


def local_loss(query_rows, key_rows, value_rows, weight_rows):
    seg_rows = query_rows.shape[0]
    scale = query_rows.shape[-1] ** (-0.5)
    causal = lax.broadcasted_iota(jnp.int32, (seg_rows, seg_rows), 0) >= lax.broadcasted_iota(
        jnp.int32, (seg_rows, seg_rows), 1
    )
    logits = jnp.einsum("sha,tha->hst", query_rows, key_rows, precision=HIGH) * scale
    logits = jnp.where(causal[None], logits, -1e30)
    top = lax.stop_gradient(jnp.max(logits, axis=2, keepdims=True))
    weights = jnp.exp(logits - top)
    local_num = jnp.einsum("hst,thb->shb", weights, value_rows, precision=HIGH)
    local_den = jnp.transpose(jnp.sum(weights, axis=2))
    from_local = local_num / local_den[:, :, None]
    return jnp.sum(weight_rows * from_local)


def memory_loss(query_rows, memory, normalizer, weight_rows):
    query_feat = feature_map(query_rows)
    retrieved = jnp.einsum("sha,hab->shb", query_feat, memory, precision=HIGH)
    denom_mem = jnp.einsum("sha,ha->sh", query_feat, normalizer, precision=HIGH) + 1.0
    return jnp.sum(weight_rows * retrieved / denom_mem[:, :, None])


def memory_slope(query_rows, normalizer, weight_rows):
    query_feat = feature_map(query_rows)
    denom_mem = jnp.einsum("sha,ha->sh", query_feat, normalizer, precision=HIGH) + 1.0
    return jnp.einsum("sha,shb->hab", query_feat, weight_rows / denom_mem[:, :, None], precision=HIGH)


def shards(features, cotangent, gate_logits, probes):
    heads = gate_logits.shape[0]
    seg_rows = features.shape[1]
    head_size = features.shape[2] // heads
    shaped = features.reshape(3, seg_rows, heads, head_size)
    query_rows, key_rows, value_rows = (shaped[0], shaped[1], shaped[2])
    cot_rows = cotangent.reshape(seg_rows, heads, head_size)
    mixing = jax.nn.sigmoid(gate_logits)[None, :, None]
    mem_weight = cot_rows * mixing
    loc_weight = cot_rows * (1.0 - mixing)
    signs = probes[0].astype(jnp.float32).reshape(3, seg_rows, heads, head_size)
    query_dir, key_dir, value_dir = (signs[0], signs[1], signs[2])
    key_feat = feature_map(key_rows)
    key_slope = feature_slope(key_rows)
    key_tan = key_slope * key_dir
    groups = lax.axis_size("probe")
    share = heads // groups
    first_head = lax.axis_index("probe") * share

    local_grad = jax.grad(local_loss, argnums=(0, 1, 2))
    _, local_curv = jax.jvp(
        lambda q, k, v: local_grad(q, k, v, loc_weight),
        (query_rows, key_rows, value_rows),
        (query_dir, key_dir, value_dir),
    )

    increment = jnp.einsum("sha,shb->hab", key_feat, value_rows, precision=HIGH)
    increment_tan = jnp.einsum("sha,shb->hab", key_tan, value_rows, precision=HIGH) + jnp.einsum(
        "sha,shb->hab", key_feat, value_dir, precision=HIGH
    )
    norm_inc = jnp.sum(key_feat, axis=0)
    norm_tan = jnp.sum(key_tan, axis=0)
    own_inc = lax.dynamic_slice_in_dim(increment, first_head, share, 0)
    own_prefix, memory_tan, norms = packed_scan(
        (own_inc, increment_tan, jnp.concatenate((norm_inc, norm_tan), axis=0)), "ctx", False
    )
    normalizer, normalizer_tan = norms[:heads], norms[heads:]
    memory = lax.all_gather(own_prefix, "probe", axis=0, tiled=True)

    slope, slope_tan = jax.jvp(
        lambda q, n: memory_slope(q, n, mem_weight), (query_rows, normalizer), (query_dir, normalizer_tan)
    )
    mem_grad = jax.grad(memory_loss, argnums=(0, 2))
    (_, back_norm_inc), (query_curv, back_norm_inc_tan) = jax.jvp(
        lambda q, m, n: mem_grad(q, m, n, mem_weight),
        (query_rows, memory, normalizer),
        (query_dir, memory_tan, normalizer_tan),
    )
    own_slope = lax.dynamic_slice_in_dim(slope, first_head, share, 0)
    own_suffix, back_mem_tan, back_norms = packed_scan(
        (own_slope, slope_tan, jnp.concatenate((back_norm_inc, back_norm_inc_tan), axis=0)), "ctx", True
    )
    back_norm, back_norm_tan = back_norms[:heads], back_norms[heads:]
    back_mem = lax.all_gather(own_suffix, "probe", axis=0, tiled=True)

    through = jnp.einsum("shb,hab->sha", value_rows, back_mem, precision=HIGH) + back_norm[None]
    through_tan = (
        jnp.einsum("shb,hab->sha", value_dir, back_mem, precision=HIGH)
        + jnp.einsum("shb,hab->sha", value_rows, back_mem_tan, precision=HIGH)
        + back_norm_tan[None]
    )
    query_out = local_curv[0] + query_curv
    key_out = local_curv[1] + feature_curve(key_rows) * key_dir * through + key_slope * through_tan
    value_out = (
        local_curv[2]
        + jnp.einsum("sha,hab->shb", key_tan, back_mem, precision=HIGH)
        + jnp.einsum("sha,hab->shb", key_feat, back_mem_tan, precision=HIGH)
    )
    stacked = jnp.stack((query_out, key_out, value_out))
    products = stacked.reshape(1, 3, seg_rows, heads * head_size)
    partial_trace = jnp.sum(signs * stacked, axis=(1, 3)) / (seg_rows * groups)
    block_trace = lax.psum(partial_trace, "probe")
    return (products, block_trace.reshape(1, 3, heads))


def solution(mesh):
    placed = (P(None, "ctx", None), P("ctx", None), P(), P("probe", None, "ctx", None))
    return jax.shard_map(
        shards,
        mesh=mesh,
        in_specs=placed,
        out_specs=(P("probe", None, "ctx", None), P("ctx", None, None)),
        check_vma=False,
    )
```

```python
import jax
import jax.numpy as jnp
from jax import lax
from jax.sharding import PartitionSpec as P

HIGH = lax.Precision.HIGH


def exclusive(block, reverse):
    count = block.shape[0]
    here = lax.broadcasted_iota(jnp.int32, (count, count), 0)
    there = lax.broadcasted_iota(jnp.int32, (count, count), 1)
    mask = (there > here) if reverse else (there < here)
    flat = block.reshape(count, -1)
    summed = jnp.dot(mask.astype(jnp.float32), flat, precision=lax.Precision.HIGHEST)
    return summed.reshape(block.shape)


def packed_scan(groups_of_parts, axis):
    count = lax.axis_size(axis)
    width = groups_of_parts[0][0][0].shape[-1]
    blocks, layout = [], []
    for parts, reverse in groups_of_parts:
        rows = [p.reshape(-1, width) for p in parts]
        sizes = [r.shape[0] for r in rows]
        total = sum(sizes)
        unit = 8 * count
        padded = -(-total // unit) * unit
        if padded > total:
            rows.append(jnp.zeros((padded - total, width), jnp.float32))
        blocks.append(jnp.concatenate(rows, axis=0).reshape(count, padded // count, width))
        layout.append((parts, sizes, padded // count, reverse))
    buffer = jnp.concatenate(blocks, axis=1) if len(blocks) > 1 else blocks[0]
    spread = lax.all_to_all(buffer, axis, 0, 0)
    scanned, offset = [], 0
    for parts, sizes, chunk, reverse in layout:
        scanned.append(exclusive(spread[:, offset:offset + chunk], reverse))
        offset += chunk
    scanned = jnp.concatenate(scanned, axis=1) if len(scanned) > 1 else scanned[0]
    back = lax.all_to_all(scanned, axis, 0, 0)
    outs, offset = [], 0
    for parts, sizes, chunk, reverse in layout:
        flat = back[:, offset:offset + chunk].reshape(count * chunk, width)
        offset += chunk
        mine, row = [], 0
        for p, size in zip(parts, sizes):
            mine.append(flat[row:row + size].reshape(p.shape))
            row += size
        outs.append(mine)
    return outs


def gathered_scan(part, axis, reverse):
    count = lax.axis_size(axis)
    place = lax.axis_index(axis)
    every = lax.all_gather(part, axis)
    source = lax.broadcasted_iota(jnp.int32, (count,) + (1,) * part.ndim, 0)
    keep = (source > place) if reverse else (source < place)
    return jnp.sum(jnp.where(keep, every, 0.0), axis=0)


def feature_map(inputs):
    return jnp.where(inputs > 0, inputs + 1.0, jnp.exp(jnp.minimum(inputs, 0.0)))


def feature_slope(inputs):
    return jnp.where(inputs > 0, 1.0, jnp.exp(jnp.minimum(inputs, 0.0)))


def feature_curve(inputs):
    return jnp.where(inputs > 0, 0.0, jnp.exp(jnp.minimum(inputs, 0.0)))


def local_loss(query_rows, key_rows, value_rows, weight_rows):
    seg_rows = query_rows.shape[0]
    scale = query_rows.shape[-1] ** (-0.5)
    causal = lax.broadcasted_iota(jnp.int32, (seg_rows, seg_rows), 0) >= lax.broadcasted_iota(
        jnp.int32, (seg_rows, seg_rows), 1
    )
    logits = jnp.einsum("sha,tha->hst", query_rows, key_rows, precision=HIGH) * scale
    logits = jnp.where(causal[None], logits, -1e30)
    top = lax.stop_gradient(jnp.max(logits, axis=2, keepdims=True))
    weights = jnp.exp(logits - top)
    local_num = jnp.einsum("hst,thb->shb", weights, value_rows, precision=HIGH)
    local_den = jnp.transpose(jnp.sum(weights, axis=2))
    from_local = local_num / local_den[:, :, None]
    return jnp.sum(weight_rows * from_local)


def memory_loss(query_rows, memory, normalizer, weight_rows):
    query_feat = feature_map(query_rows)
    retrieved = jnp.einsum("sha,hab->shb", query_feat, memory, precision=HIGH)
    denom_mem = jnp.einsum("sha,ha->sh", query_feat, normalizer, precision=HIGH) + 1.0
    return jnp.sum(weight_rows * retrieved / denom_mem[:, :, None])


def memory_slope(query_rows, normalizer, weight_rows):
    query_feat = feature_map(query_rows)
    denom_mem = jnp.einsum("sha,ha->sh", query_feat, normalizer, precision=HIGH) + 1.0
    return jnp.einsum("sha,shb->hab", query_feat, weight_rows / denom_mem[:, :, None], precision=HIGH)


def shards(features, cotangent, gate_logits, probes):
    heads = gate_logits.shape[0]
    seg_rows = features.shape[1]
    head_size = features.shape[2] // heads
    shaped = features.reshape(3, seg_rows, heads, head_size)
    query_rows, key_rows, value_rows = (shaped[0], shaped[1], shaped[2])
    cot_rows = cotangent.reshape(seg_rows, heads, head_size)
    mixing = jax.nn.sigmoid(gate_logits)[None, :, None]
    mem_weight = cot_rows * mixing
    loc_weight = cot_rows * (1.0 - mixing)
    signs = probes[0].astype(jnp.float32).reshape(3, seg_rows, heads, head_size)
    query_dir, key_dir, value_dir = (signs[0], signs[1], signs[2])
    key_feat = feature_map(key_rows)
    key_slope = feature_slope(key_rows)
    key_tan = key_slope * key_dir
    groups = lax.axis_size("probe")
    share = heads // groups
    first_head = lax.axis_index("probe") * share

    local_grad = jax.grad(local_loss, argnums=(0, 1, 2))
    _, local_curv = jax.jvp(
        lambda q, k, v: local_grad(q, k, v, loc_weight),
        (query_rows, key_rows, value_rows),
        (query_dir, key_dir, value_dir),
    )

    norms = gathered_scan(jnp.concatenate((jnp.sum(key_feat, axis=0), jnp.sum(key_tan, axis=0)), axis=0), "ctx", False)
    normalizer, normalizer_tan = norms[:heads], norms[heads:]

    increment = jnp.einsum("sha,shb->hab", key_feat, value_rows, precision=HIGH)
    increment_tan = jnp.einsum("sha,shb->hab", key_tan, value_rows, precision=HIGH) + jnp.einsum(
        "sha,shb->hab", key_feat, value_dir, precision=HIGH
    )
    slope, slope_tan = jax.jvp(
        lambda q, n: memory_slope(q, n, mem_weight), (query_rows, normalizer), (query_dir, normalizer_tan)
    )
    own_inc = lax.dynamic_slice_in_dim(increment, first_head, share, 0)
    own_slope = lax.dynamic_slice_in_dim(slope, first_head, share, 0)
    (own_prefix, memory_tan), (own_suffix, back_mem_tan) = packed_scan(
        [((own_inc, increment_tan), False), ((own_slope, slope_tan), True)], "ctx"
    )
    both = lax.all_gather(jnp.stack((own_prefix, own_suffix)), "probe", axis=1, tiled=True)
    memory, back_mem = both[0], both[1]

    mem_grad = jax.grad(memory_loss, argnums=(0, 2))
    (_, back_norm_inc), (query_curv, back_norm_inc_tan) = jax.jvp(
        lambda q, m, n: mem_grad(q, m, n, mem_weight),
        (query_rows, memory, normalizer),
        (query_dir, memory_tan, normalizer_tan),
    )
    back_norms = gathered_scan(jnp.concatenate((back_norm_inc, back_norm_inc_tan), axis=0), "ctx", True)
    back_norm, back_norm_tan = back_norms[:heads], back_norms[heads:]

    through = jnp.einsum("shb,hab->sha", value_rows, back_mem, precision=HIGH) + back_norm[None]
    through_tan = (
        jnp.einsum("shb,hab->sha", value_dir, back_mem, precision=HIGH)
        + jnp.einsum("shb,hab->sha", value_rows, back_mem_tan, precision=HIGH)
        + back_norm_tan[None]
    )
    query_out = local_curv[0] + query_curv
    key_out = local_curv[1] + feature_curve(key_rows) * key_dir * through + key_slope * through_tan
    value_out = (
        local_curv[2]
        + jnp.einsum("sha,hab->shb", key_tan, back_mem, precision=HIGH)
        + jnp.einsum("sha,hab->shb", key_feat, back_mem_tan, precision=HIGH)
    )
    stacked = jnp.stack((query_out, key_out, value_out))
    products = stacked.reshape(1, 3, seg_rows, heads * head_size)
    partial_trace = jnp.sum(signs * stacked, axis=(1, 3)) / (seg_rows * groups)
    block_trace = lax.psum(partial_trace, "probe")
    return (products, block_trace.reshape(1, 3, heads))


def solution(mesh):
    placed = (P(None, "ctx", None), P("ctx", None), P(), P("probe", None, "ctx", None))
    return jax.shard_map(
        shards,
        mesh=mesh,
        in_specs=placed,
        out_specs=(P("probe", None, "ctx", None), P("ctx", None, None)),
        check_vma=False,
    )
```

```python
import jax
import jax.numpy as jnp
from jax import lax
from jax.sharding import PartitionSpec as P

HIGH = lax.Precision.HIGH


def exclusive(block, reverse):
    count = block.shape[0]
    here = lax.broadcasted_iota(jnp.int32, (count, count), 0)
    there = lax.broadcasted_iota(jnp.int32, (count, count), 1)
    mask = (there > here) if reverse else (there < here)
    flat = block.reshape(count, -1)
    summed = jnp.dot(mask.astype(jnp.float32), flat, precision=lax.Precision.HIGHEST)
    return summed.reshape(block.shape)


def packed_scan(parts, axis, reverse, cover=None, cover_args=()):
    count = lax.axis_size(axis)
    width = parts[0].shape[-1]
    rows = [p.reshape(-1, width) for p in parts]
    sizes = [r.shape[0] for r in rows]
    total = sum(sizes)
    unit = 8 * count
    padded = -(-total // unit) * unit
    if padded > total:
        rows.append(jnp.zeros((padded - total, width), jnp.float32))
    buffer = jnp.concatenate(rows, axis=0).reshape(count, padded // count, width)
    covered = None
    if cover is not None:
        buffer, cover_args = lax.optimization_barrier((buffer, cover_args))
    spread = lax.all_to_all(buffer, axis, 0, 0)
    if cover is not None:
        covered = cover(*cover_args)
        spread, covered = lax.optimization_barrier((spread, covered))
    back = lax.all_to_all(exclusive(spread, reverse), axis, 0, 0).reshape(padded, width)
    outs, row = [], 0
    for p, size in zip(parts, sizes):
        outs.append(back[row:row + size].reshape(p.shape))
        row += size
    return outs, covered


def feature_map(inputs):
    return jnp.where(inputs > 0, inputs + 1.0, jnp.exp(jnp.minimum(inputs, 0.0)))


def feature_slope(inputs):
    return jnp.where(inputs > 0, 1.0, jnp.exp(jnp.minimum(inputs, 0.0)))


def feature_curve(inputs):
    return jnp.where(inputs > 0, 0.0, jnp.exp(jnp.minimum(inputs, 0.0)))


def local_loss(query_rows, key_rows, value_rows, weight_rows):
    seg_rows = query_rows.shape[0]
    scale = query_rows.shape[-1] ** (-0.5)
    causal = lax.broadcasted_iota(jnp.int32, (seg_rows, seg_rows), 0) >= lax.broadcasted_iota(
        jnp.int32, (seg_rows, seg_rows), 1
    )
    logits = jnp.einsum("sha,tha->hst", query_rows, key_rows, precision=HIGH) * scale
    logits = jnp.where(causal[None], logits, -1e30)
    top = lax.stop_gradient(jnp.max(logits, axis=2, keepdims=True))
    weights = jnp.exp(logits - top)
    local_num = jnp.einsum("hst,thb->shb", weights, value_rows, precision=HIGH)
    local_den = jnp.transpose(jnp.sum(weights, axis=2))
    from_local = local_num / local_den[:, :, None]
    return jnp.sum(weight_rows * from_local)


def memory_loss(query_rows, memory, normalizer, weight_rows):
    query_feat = feature_map(query_rows)
    retrieved = jnp.einsum("sha,hab->shb", query_feat, memory, precision=HIGH)
    denom_mem = jnp.einsum("sha,ha->sh", query_feat, normalizer, precision=HIGH) + 1.0
    return jnp.sum(weight_rows * retrieved / denom_mem[:, :, None])


def memory_slope(query_rows, normalizer, weight_rows):
    query_feat = feature_map(query_rows)
    denom_mem = jnp.einsum("sha,ha->sh", query_feat, normalizer, precision=HIGH) + 1.0
    return jnp.einsum("sha,shb->hab", query_feat, weight_rows / denom_mem[:, :, None], precision=HIGH)


def shards(features, cotangent, gate_logits, probes):
    heads = gate_logits.shape[0]
    seg_rows = features.shape[1]
    head_size = features.shape[2] // heads
    shaped = features.reshape(3, seg_rows, heads, head_size)
    query_rows, key_rows, value_rows = (shaped[0], shaped[1], shaped[2])
    cot_rows = cotangent.reshape(seg_rows, heads, head_size)
    mixing = jax.nn.sigmoid(gate_logits)[None, :, None]
    mem_weight = cot_rows * mixing
    loc_weight = cot_rows * (1.0 - mixing)
    signs = probes[0].astype(jnp.float32).reshape(3, seg_rows, heads, head_size)
    query_dir, key_dir, value_dir = (signs[0], signs[1], signs[2])
    key_feat = feature_map(key_rows)
    key_slope = feature_slope(key_rows)
    key_tan = key_slope * key_dir
    groups = lax.axis_size("probe")
    share = heads // groups
    first_head = lax.axis_index("probe") * share

    local_grad = jax.grad(local_loss, argnums=(0, 1, 2))

    def local_part(q, k, v, dq, dk, dv, w):
        return jax.jvp(lambda a, b, c: local_grad(a, b, c, w), (q, k, v), (dq, dk, dv))[1]

    increment = jnp.einsum("sha,shb->hab", key_feat, value_rows, precision=HIGH)
    increment_tan = jnp.einsum("sha,shb->hab", key_tan, value_rows, precision=HIGH) + jnp.einsum(
        "sha,shb->hab", key_feat, value_dir, precision=HIGH
    )
    norm_inc = jnp.sum(key_feat, axis=0)
    norm_tan = jnp.sum(key_tan, axis=0)
    own_inc = lax.dynamic_slice_in_dim(increment, first_head, share, 0)
    (own_prefix, memory_tan, norms), local_curv = packed_scan(
        (own_inc, increment_tan, jnp.concatenate((norm_inc, norm_tan), axis=0)),
        "ctx",
        False,
        local_part,
        (query_rows, key_rows, value_rows, query_dir, key_dir, value_dir, loc_weight),
    )
    normalizer, normalizer_tan = norms[:heads], norms[heads:]
    memory = lax.all_gather(own_prefix, "probe", axis=0, tiled=True)

    slope, slope_tan = jax.jvp(
        lambda q, n: memory_slope(q, n, mem_weight), (query_rows, normalizer), (query_dir, normalizer_tan)
    )
    mem_grad = jax.grad(memory_loss, argnums=(0, 2))
    (_, back_norm_inc), (query_curv, back_norm_inc_tan) = jax.jvp(
        lambda q, m, n: mem_grad(q, m, n, mem_weight),
        (query_rows, memory, normalizer),
        (query_dir, memory_tan, normalizer_tan),
    )
    own_slope = lax.dynamic_slice_in_dim(slope, first_head, share, 0)
    (own_suffix, back_mem_tan, back_norms), _ = packed_scan(
        (own_slope, slope_tan, jnp.concatenate((back_norm_inc, back_norm_inc_tan), axis=0)), "ctx", True
    )
    back_norm, back_norm_tan = back_norms[:heads], back_norms[heads:]
    back_mem = lax.all_gather(own_suffix, "probe", axis=0, tiled=True)

    through = jnp.einsum("shb,hab->sha", value_rows, back_mem, precision=HIGH) + back_norm[None]
    through_tan = (
        jnp.einsum("shb,hab->sha", value_dir, back_mem, precision=HIGH)
        + jnp.einsum("shb,hab->sha", value_rows, back_mem_tan, precision=HIGH)
        + back_norm_tan[None]
    )
    query_out = local_curv[0] + query_curv
    key_out = local_curv[1] + feature_curve(key_rows) * key_dir * through + key_slope * through_tan
    value_out = (
        local_curv[2]
        + jnp.einsum("sha,hab->shb", key_tan, back_mem, precision=HIGH)
        + jnp.einsum("sha,hab->shb", key_feat, back_mem_tan, precision=HIGH)
    )
    stacked = jnp.stack((query_out, key_out, value_out))
    products = stacked.reshape(1, 3, seg_rows, heads * head_size)
    partial_trace = jnp.sum(signs * stacked, axis=(1, 3)) / (seg_rows * groups)
    block_trace = lax.psum(partial_trace, "probe")
    return (products, block_trace.reshape(1, 3, heads))


def solution(mesh):
    placed = (P(None, "ctx", None), P("ctx", None), P(), P("probe", None, "ctx", None))
    return jax.shard_map(
        shards,
        mesh=mesh,
        in_specs=placed,
        out_specs=(P("probe", None, "ctx", None), P("ctx", None, None)),
        check_vma=False,
    )
```

```python
import jax
import jax.numpy as jnp
from jax import lax
from jax.sharding import PartitionSpec as P

HIGH = lax.Precision.HIGH
CTX = ("outer", "inner")


def exclusive(block, reverse):
    count = block.shape[0]
    here = lax.broadcasted_iota(jnp.int32, (count, count), 0)
    there = lax.broadcasted_iota(jnp.int32, (count, count), 1)
    mask = (there > here) if reverse else (there < here)
    flat = block.reshape(count, -1)
    summed = jnp.dot(mask.astype(jnp.float32), flat, precision=lax.Precision.HIGHEST)
    return summed.reshape(block.shape)


def outer_exclusive(total, axis, reverse):
    count = lax.axis_size(axis)
    step = -1 if reverse else 1

    def shifted(value, by):
        pairs = [(i, i + step * by) for i in range(count) if 0 <= i + step * by < count]
        return lax.ppermute(value, axis, pairs)

    if count == 1:
        return jnp.zeros_like(total)
    acc = shifted(total, 1)
    by = 1
    while by < count - 1:
        acc = acc + shifted(acc, by)
        by *= 2
    return acc


def packed_scan(parts, axis, reverse):
    outer, inner = axis
    count = lax.axis_size(inner)
    width = parts[0].shape[-1]
    rows = [p.reshape(-1, width) for p in parts]
    sizes = [r.shape[0] for r in rows]
    total = sum(sizes)
    unit = 8 * count
    padded = -(-total // unit) * unit
    if padded > total:
        rows.append(jnp.zeros((padded - total, width), jnp.float32))
    buffer = jnp.concatenate(rows, axis=0).reshape(count, padded // count, width)
    spread = lax.all_to_all(buffer, inner, 0, 0)
    carry = outer_exclusive(jnp.sum(spread, axis=0), outer, reverse)
    scanned = exclusive(spread, reverse) + carry[None]
    back = lax.all_to_all(scanned, inner, 0, 0).reshape(padded, width)
    outs, row = [], 0
    for p, size in zip(parts, sizes):
        outs.append(back[row:row + size].reshape(p.shape))
        row += size
    return outs


def feature_map(inputs):
    return jnp.where(inputs > 0, inputs + 1.0, jnp.exp(jnp.minimum(inputs, 0.0)))


def feature_slope(inputs):
    return jnp.where(inputs > 0, 1.0, jnp.exp(jnp.minimum(inputs, 0.0)))


def feature_curve(inputs):
    return jnp.where(inputs > 0, 0.0, jnp.exp(jnp.minimum(inputs, 0.0)))


def local_loss(query_rows, key_rows, value_rows, weight_rows):
    seg_rows = query_rows.shape[0]
    scale = query_rows.shape[-1] ** (-0.5)
    causal = lax.broadcasted_iota(jnp.int32, (seg_rows, seg_rows), 0) >= lax.broadcasted_iota(
        jnp.int32, (seg_rows, seg_rows), 1
    )
    logits = jnp.einsum("sha,tha->hst", query_rows, key_rows, precision=HIGH) * scale
    logits = jnp.where(causal[None], logits, -1e30)
    top = lax.stop_gradient(jnp.max(logits, axis=2, keepdims=True))
    weights = jnp.exp(logits - top)
    local_num = jnp.einsum("hst,thb->shb", weights, value_rows, precision=HIGH)
    local_den = jnp.transpose(jnp.sum(weights, axis=2))
    from_local = local_num / local_den[:, :, None]
    return jnp.sum(weight_rows * from_local)


def memory_loss(query_rows, memory, normalizer, weight_rows):
    query_feat = feature_map(query_rows)
    retrieved = jnp.einsum("sha,hab->shb", query_feat, memory, precision=HIGH)
    denom_mem = jnp.einsum("sha,ha->sh", query_feat, normalizer, precision=HIGH) + 1.0
    return jnp.sum(weight_rows * retrieved / denom_mem[:, :, None])


def memory_slope(query_rows, normalizer, weight_rows):
    query_feat = feature_map(query_rows)
    denom_mem = jnp.einsum("sha,ha->sh", query_feat, normalizer, precision=HIGH) + 1.0
    return jnp.einsum("sha,shb->hab", query_feat, weight_rows / denom_mem[:, :, None], precision=HIGH)


def shards(features, cotangent, gate_logits, probes):
    heads = gate_logits.shape[0]
    seg_rows = features.shape[1]
    head_size = features.shape[2] // heads
    shaped = features.reshape(3, seg_rows, heads, head_size)
    query_rows, key_rows, value_rows = (shaped[0], shaped[1], shaped[2])
    cot_rows = cotangent.reshape(seg_rows, heads, head_size)
    mixing = jax.nn.sigmoid(gate_logits)[None, :, None]
    mem_weight = cot_rows * mixing
    loc_weight = cot_rows * (1.0 - mixing)
    signs = probes[0].astype(jnp.float32).reshape(3, seg_rows, heads, head_size)
    query_dir, key_dir, value_dir = (signs[0], signs[1], signs[2])
    key_feat = feature_map(key_rows)
    key_slope = feature_slope(key_rows)
    key_tan = key_slope * key_dir
    groups = lax.axis_size("probe")
    share = heads // groups
    first_head = lax.axis_index("probe") * share

    local_grad = jax.grad(local_loss, argnums=(0, 1, 2))
    _, local_curv = jax.jvp(
        lambda q, k, v: local_grad(q, k, v, loc_weight),
        (query_rows, key_rows, value_rows),
        (query_dir, key_dir, value_dir),
    )

    increment = jnp.einsum("sha,shb->hab", key_feat, value_rows, precision=HIGH)
    increment_tan = jnp.einsum("sha,shb->hab", key_tan, value_rows, precision=HIGH) + jnp.einsum(
        "sha,shb->hab", key_feat, value_dir, precision=HIGH
    )
    norm_inc = jnp.sum(key_feat, axis=0)
    norm_tan = jnp.sum(key_tan, axis=0)
    own_inc = lax.dynamic_slice_in_dim(increment, first_head, share, 0)
    own_prefix, memory_tan, norms = packed_scan(
        (own_inc, increment_tan, jnp.concatenate((norm_inc, norm_tan), axis=0)), CTX, False
    )
    normalizer, normalizer_tan = norms[:heads], norms[heads:]
    memory = lax.all_gather(own_prefix, "probe", axis=0, tiled=True)

    slope, slope_tan = jax.jvp(
        lambda q, n: memory_slope(q, n, mem_weight), (query_rows, normalizer), (query_dir, normalizer_tan)
    )
    mem_grad = jax.grad(memory_loss, argnums=(0, 2))
    (_, back_norm_inc), (query_curv, back_norm_inc_tan) = jax.jvp(
        lambda q, m, n: mem_grad(q, m, n, mem_weight),
        (query_rows, memory, normalizer),
        (query_dir, memory_tan, normalizer_tan),
    )
    own_slope = lax.dynamic_slice_in_dim(slope, first_head, share, 0)
    own_suffix, back_mem_tan, back_norms = packed_scan(
        (own_slope, slope_tan, jnp.concatenate((back_norm_inc, back_norm_inc_tan), axis=0)), CTX, True
    )
    back_norm, back_norm_tan = back_norms[:heads], back_norms[heads:]
    back_mem = lax.all_gather(own_suffix, "probe", axis=0, tiled=True)

    through = jnp.einsum("shb,hab->sha", value_rows, back_mem, precision=HIGH) + back_norm[None]
    through_tan = (
        jnp.einsum("shb,hab->sha", value_dir, back_mem, precision=HIGH)
        + jnp.einsum("shb,hab->sha", value_rows, back_mem_tan, precision=HIGH)
        + back_norm_tan[None]
    )
    query_out = local_curv[0] + query_curv
    key_out = local_curv[1] + feature_curve(key_rows) * key_dir * through + key_slope * through_tan
    value_out = (
        local_curv[2]
        + jnp.einsum("sha,hab->shb", key_tan, back_mem, precision=HIGH)
        + jnp.einsum("sha,hab->shb", key_feat, back_mem_tan, precision=HIGH)
    )
    stacked = jnp.stack((query_out, key_out, value_out))
    products = stacked.reshape(1, 3, seg_rows, heads * head_size)
    partial_trace = jnp.sum(signs * stacked, axis=(1, 3)) / (seg_rows * groups)
    block_trace = lax.psum(partial_trace, "probe")
    return (products, block_trace.reshape(1, 3, heads))


def solution(mesh):
    ctx = mesh.shape["ctx"]
    inner = 4 if ctx % 4 == 0 else ctx
    devices = mesh.devices.reshape(ctx // inner, inner, mesh.shape["probe"])
    split = jax.sharding.Mesh(devices, ("outer", "inner", "probe"))
    placed = (P(None, CTX, None), P(CTX, None), P(), P("probe", None, CTX, None))
    return jax.shard_map(
        shards,
        mesh=split,
        in_specs=placed,
        out_specs=(P("probe", None, CTX, None), P(CTX, None, None)),
        check_vma=False,
    )
```

```python
import jax
import jax.numpy as jnp
from jax import lax
from jax.sharding import PartitionSpec as P

HIGH = lax.Precision.HIGH
CTX = ("outer", "inner")


def exclusive(block, reverse):
    count = block.shape[0]
    here = lax.broadcasted_iota(jnp.int32, (count, count), 0)
    there = lax.broadcasted_iota(jnp.int32, (count, count), 1)
    mask = (there > here) if reverse else (there < here)
    flat = block.reshape(count, -1)
    summed = jnp.dot(mask.astype(jnp.float32), flat, precision=lax.Precision.HIGHEST)
    return summed.reshape(block.shape)


def outer_exclusive(total, axis, reverse):
    count = lax.axis_size(axis)
    step = -1 if reverse else 1

    def shifted(value, by):
        pairs = [(i, i + step * by) for i in range(count) if 0 <= i + step * by < count]
        return lax.ppermute(value, axis, pairs)

    if count == 1:
        return jnp.zeros_like(total)
    acc = shifted(total, 1)
    by = 1
    while by < count - 1:
        acc = acc + shifted(acc, by)
        by *= 2
    return acc


def packed_scan(parts, axis, reverse):
    outer, inner = axis
    count = lax.axis_size(inner)
    width = parts[0].shape[-1]
    rows = [p.reshape(-1, width) for p in parts]
    sizes = [r.shape[0] for r in rows]
    total = sum(sizes)
    unit = 8 * count
    padded = -(-total // unit) * unit
    if padded > total:
        rows.append(jnp.zeros((padded - total, width), jnp.float32))
    buffer = jnp.concatenate(rows, axis=0).reshape(count, padded // count, width)
    spread = lax.all_to_all(buffer, inner, 0, 0)
    carry = outer_exclusive(jnp.sum(spread, axis=0), outer, reverse)
    scanned = exclusive(spread, reverse) + carry[None]
    back = lax.all_to_all(scanned, inner, 0, 0).reshape(padded, width)
    outs, row = [], 0
    for p, size in zip(parts, sizes):
        outs.append(back[row:row + size].reshape(p.shape))
        row += size
    return outs


def reduced_scan(part, axis, reverse):
    count = lax.axis_size(axis)
    place = lax.axis_index(axis)
    slot = lax.broadcasted_iota(jnp.int32, (count,) + (1,) * part.ndim, 0)
    every = lax.psum(jnp.where(slot == place, part[None], 0.0), axis)
    keep = (slot > place) if reverse else (slot < place)
    return jnp.sum(jnp.where(keep, every, 0.0), axis=0)


def feature_map(inputs):
    return jnp.where(inputs > 0, inputs + 1.0, jnp.exp(jnp.minimum(inputs, 0.0)))


def feature_slope(inputs):
    return jnp.where(inputs > 0, 1.0, jnp.exp(jnp.minimum(inputs, 0.0)))


def feature_curve(inputs):
    return jnp.where(inputs > 0, 0.0, jnp.exp(jnp.minimum(inputs, 0.0)))


def local_loss(query_rows, key_rows, value_rows, weight_rows):
    seg_rows = query_rows.shape[0]
    scale = query_rows.shape[-1] ** (-0.5)
    causal = lax.broadcasted_iota(jnp.int32, (seg_rows, seg_rows), 0) >= lax.broadcasted_iota(
        jnp.int32, (seg_rows, seg_rows), 1
    )
    logits = jnp.einsum("sha,tha->hst", query_rows, key_rows, precision=HIGH) * scale
    logits = jnp.where(causal[None], logits, -1e30)
    top = lax.stop_gradient(jnp.max(logits, axis=2, keepdims=True))
    weights = jnp.exp(logits - top)
    local_num = jnp.einsum("hst,thb->shb", weights, value_rows, precision=HIGH)
    local_den = jnp.transpose(jnp.sum(weights, axis=2))
    from_local = local_num / local_den[:, :, None]
    return jnp.sum(weight_rows * from_local)


def memory_loss(query_rows, memory, normalizer, weight_rows):
    query_feat = feature_map(query_rows)
    retrieved = jnp.einsum("sha,hab->shb", query_feat, memory, precision=HIGH)
    denom_mem = jnp.einsum("sha,ha->sh", query_feat, normalizer, precision=HIGH) + 1.0
    return jnp.sum(weight_rows * retrieved / denom_mem[:, :, None])


def memory_slope(query_rows, normalizer, weight_rows):
    query_feat = feature_map(query_rows)
    denom_mem = jnp.einsum("sha,ha->sh", query_feat, normalizer, precision=HIGH) + 1.0
    return jnp.einsum("sha,shb->hab", query_feat, weight_rows / denom_mem[:, :, None], precision=HIGH)


def shards(features, cotangent, gate_logits, probes):
    heads = gate_logits.shape[0]
    seg_rows = features.shape[1]
    head_size = features.shape[2] // heads
    shaped = features.reshape(3, seg_rows, heads, head_size)
    query_rows, key_rows, value_rows = (shaped[0], shaped[1], shaped[2])
    cot_rows = cotangent.reshape(seg_rows, heads, head_size)
    mixing = jax.nn.sigmoid(gate_logits)[None, :, None]
    mem_weight = cot_rows * mixing
    loc_weight = cot_rows * (1.0 - mixing)
    signs = probes[0].astype(jnp.float32).reshape(3, seg_rows, heads, head_size)
    query_dir, key_dir, value_dir = (signs[0], signs[1], signs[2])
    key_feat = feature_map(key_rows)
    key_slope = feature_slope(key_rows)
    key_tan = key_slope * key_dir
    groups = lax.axis_size("probe")
    share = heads // groups
    first_head = lax.axis_index("probe") * share

    local_grad = jax.grad(local_loss, argnums=(0, 1, 2))
    _, local_curv = jax.jvp(
        lambda q, k, v: local_grad(q, k, v, loc_weight),
        (query_rows, key_rows, value_rows),
        (query_dir, key_dir, value_dir),
    )

    increment = jnp.einsum("sha,shb->hab", key_feat, value_rows, precision=HIGH)
    increment_tan = jnp.einsum("sha,shb->hab", key_tan, value_rows, precision=HIGH) + jnp.einsum(
        "sha,shb->hab", key_feat, value_dir, precision=HIGH
    )
    norm_inc = jnp.sum(key_feat, axis=0)
    norm_tan = jnp.sum(key_tan, axis=0)
    own_inc = lax.dynamic_slice_in_dim(increment, first_head, share, 0)
    own_prefix, memory_tan, norms = packed_scan(
        (own_inc, increment_tan, jnp.concatenate((norm_inc, norm_tan), axis=0)), CTX, False
    )
    normalizer, normalizer_tan = norms[:heads], norms[heads:]
    memory = lax.all_gather(own_prefix, "probe", axis=0, tiled=True)

    slope, slope_tan = jax.jvp(
        lambda q, n: memory_slope(q, n, mem_weight), (query_rows, normalizer), (query_dir, normalizer_tan)
    )
    own_slope = lax.dynamic_slice_in_dim(slope, first_head, share, 0)
    own_suffix, back_mem_tan = packed_scan((own_slope, slope_tan), CTX, True)
    back_mem = lax.all_gather(own_suffix, "probe", axis=0, tiled=True)

    mem_grad = jax.grad(memory_loss, argnums=(0, 2))
    (_, back_norm_inc), (query_curv, back_norm_inc_tan) = jax.jvp(
        lambda q, m, n: mem_grad(q, m, n, mem_weight),
        (query_rows, memory, normalizer),
        (query_dir, memory_tan, normalizer_tan),
    )
    back_norms = reduced_scan(jnp.concatenate((back_norm_inc, back_norm_inc_tan), axis=0), CTX, True)
    back_norm, back_norm_tan = back_norms[:heads], back_norms[heads:]

    through = jnp.einsum("shb,hab->sha", value_rows, back_mem, precision=HIGH) + back_norm[None]
    through_tan = (
        jnp.einsum("shb,hab->sha", value_dir, back_mem, precision=HIGH)
        + jnp.einsum("shb,hab->sha", value_rows, back_mem_tan, precision=HIGH)
        + back_norm_tan[None]
    )
    query_out = local_curv[0] + query_curv
    key_out = local_curv[1] + feature_curve(key_rows) * key_dir * through + key_slope * through_tan
    value_out = (
        local_curv[2]
        + jnp.einsum("sha,hab->shb", key_tan, back_mem, precision=HIGH)
        + jnp.einsum("sha,hab->shb", key_feat, back_mem_tan, precision=HIGH)
    )
    stacked = jnp.stack((query_out, key_out, value_out))
    products = stacked.reshape(1, 3, seg_rows, heads * head_size)
    partial_trace = jnp.sum(signs * stacked, axis=(1, 3)) / (seg_rows * groups)
    block_trace = lax.psum(partial_trace, "probe")
    return (products, block_trace.reshape(1, 3, heads))


def solution(mesh):
    ctx = mesh.shape["ctx"]
    inner = 4 if ctx % 4 == 0 else ctx
    devices = mesh.devices.reshape(ctx // inner, inner, mesh.shape["probe"])
    split = jax.sharding.Mesh(devices, ("outer", "inner", "probe"))
    placed = (P(None, CTX, None), P(CTX, None), P(), P("probe", None, CTX, None))
    return jax.shard_map(
        shards,
        mesh=split,
        in_specs=placed,
        out_specs=(P("probe", None, CTX, None), P(CTX, None, None)),
        check_vma=False,
    )
```

```python
import jax
import jax.numpy as jnp
from jax import lax
from jax.sharding import PartitionSpec as P

HIGH = lax.Precision.HIGH
CTX = ("outer", "inner")


def exclusive(block, reverse):
    count = block.shape[0]
    here = lax.broadcasted_iota(jnp.int32, (count, count), 0)
    there = lax.broadcasted_iota(jnp.int32, (count, count), 1)
    mask = (there > here) if reverse else (there < here)
    flat = block.reshape(count, -1)
    summed = jnp.dot(mask.astype(jnp.float32), flat, precision=lax.Precision.HIGHEST)
    return summed.reshape(block.shape)


def outer_exclusive(total, axis, reverse):
    count = lax.axis_size(axis)
    step = -1 if reverse else 1

    def shifted(value, by):
        pairs = [(i, i + step * by) for i in range(count) if 0 <= i + step * by < count]
        return lax.ppermute(value, axis, pairs)

    if count == 1:
        return jnp.zeros_like(total)
    acc = shifted(total, 1)
    by = 1
    while by < count - 1:
        acc = acc + shifted(acc, by)
        by *= 2
    return acc


def packed_scan(parts, axis, reverse):
    outer, inner = axis
    count = lax.axis_size(inner)
    width = parts[0].shape[-1]
    rows = [p.reshape(-1, width) for p in parts]
    sizes = [r.shape[0] for r in rows]
    total = sum(sizes)
    unit = 8 * count
    padded = -(-total // unit) * unit
    if padded > total:
        rows.append(jnp.zeros((padded - total, width), jnp.float32))
    buffer = jnp.concatenate(rows, axis=0).reshape(count, padded // count, width)
    spread = lax.all_to_all(buffer, inner, 0, 0)
    carry = outer_exclusive(jnp.sum(spread, axis=0), outer, reverse)
    scanned = exclusive(spread, reverse) + carry[None]
    back = lax.all_to_all(scanned, inner, 0, 0).reshape(padded, width)
    outs, row = [], 0
    for p, size in zip(parts, sizes):
        outs.append(back[row:row + size].reshape(p.shape))
        row += size
    return outs


def reduced_scan(part, axis, reverse):
    count = lax.axis_size(axis)
    place = lax.axis_index(axis)
    slot = lax.broadcasted_iota(jnp.int32, (count,) + (1,) * part.ndim, 0)
    every = lax.all_to_all(jnp.broadcast_to(part[None], (count,) + part.shape), axis, 0, 0)
    keep = (slot > place) if reverse else (slot < place)
    return jnp.sum(jnp.where(keep, every, 0.0), axis=0)


def feature_map(inputs):
    return jnp.where(inputs > 0, inputs + 1.0, jnp.exp(jnp.minimum(inputs, 0.0)))


def feature_slope(inputs):
    return jnp.where(inputs > 0, 1.0, jnp.exp(jnp.minimum(inputs, 0.0)))


def feature_curve(inputs):
    return jnp.where(inputs > 0, 0.0, jnp.exp(jnp.minimum(inputs, 0.0)))


def local_loss(query_rows, key_rows, value_rows, weight_rows):
    seg_rows = query_rows.shape[0]
    scale = query_rows.shape[-1] ** (-0.5)
    causal = lax.broadcasted_iota(jnp.int32, (seg_rows, seg_rows), 0) >= lax.broadcasted_iota(
        jnp.int32, (seg_rows, seg_rows), 1
    )
    logits = jnp.einsum("sha,tha->hst", query_rows, key_rows, precision=HIGH) * scale
    logits = jnp.where(causal[None], logits, -1e30)
    top = lax.stop_gradient(jnp.max(logits, axis=2, keepdims=True))
    weights = jnp.exp(logits - top)
    local_num = jnp.einsum("hst,thb->shb", weights, value_rows, precision=HIGH)
    local_den = jnp.transpose(jnp.sum(weights, axis=2))
    from_local = local_num / local_den[:, :, None]
    return jnp.sum(weight_rows * from_local)


def memory_loss(query_rows, memory, normalizer, weight_rows):
    query_feat = feature_map(query_rows)
    retrieved = jnp.einsum("sha,hab->shb", query_feat, memory, precision=HIGH)
    denom_mem = jnp.einsum("sha,ha->sh", query_feat, normalizer, precision=HIGH) + 1.0
    return jnp.sum(weight_rows * retrieved / denom_mem[:, :, None])


def memory_slope(query_rows, normalizer, weight_rows):
    query_feat = feature_map(query_rows)
    denom_mem = jnp.einsum("sha,ha->sh", query_feat, normalizer, precision=HIGH) + 1.0
    return jnp.einsum("sha,shb->hab", query_feat, weight_rows / denom_mem[:, :, None], precision=HIGH)


def shards(features, cotangent, gate_logits, probes):
    heads = gate_logits.shape[0]
    seg_rows = features.shape[1]
    head_size = features.shape[2] // heads
    shaped = features.reshape(3, seg_rows, heads, head_size)
    query_rows, key_rows, value_rows = (shaped[0], shaped[1], shaped[2])
    cot_rows = cotangent.reshape(seg_rows, heads, head_size)
    mixing = jax.nn.sigmoid(gate_logits)[None, :, None]
    mem_weight = cot_rows * mixing
    loc_weight = cot_rows * (1.0 - mixing)
    signs = probes[0].astype(jnp.float32).reshape(3, seg_rows, heads, head_size)
    query_dir, key_dir, value_dir = (signs[0], signs[1], signs[2])
    key_feat = feature_map(key_rows)
    key_slope = feature_slope(key_rows)
    key_tan = key_slope * key_dir
    groups = lax.axis_size("probe")
    share = heads // groups
    first_head = lax.axis_index("probe") * share

    local_grad = jax.grad(local_loss, argnums=(0, 1, 2))
    _, local_curv = jax.jvp(
        lambda q, k, v: local_grad(q, k, v, loc_weight),
        (query_rows, key_rows, value_rows),
        (query_dir, key_dir, value_dir),
    )

    increment = jnp.einsum("sha,shb->hab", key_feat, value_rows, precision=HIGH)
    increment_tan = jnp.einsum("sha,shb->hab", key_tan, value_rows, precision=HIGH) + jnp.einsum(
        "sha,shb->hab", key_feat, value_dir, precision=HIGH
    )
    norm_inc = jnp.sum(key_feat, axis=0)
    norm_tan = jnp.sum(key_tan, axis=0)
    own_inc = lax.dynamic_slice_in_dim(increment, first_head, share, 0)
    own_prefix, memory_tan, norms = packed_scan(
        (own_inc, increment_tan, jnp.concatenate((norm_inc, norm_tan), axis=0)), CTX, False
    )
    normalizer, normalizer_tan = norms[:heads], norms[heads:]
    memory = lax.all_gather(own_prefix, "probe", axis=0, tiled=True)

    slope, slope_tan = jax.jvp(
        lambda q, n: memory_slope(q, n, mem_weight), (query_rows, normalizer), (query_dir, normalizer_tan)
    )
    own_slope = lax.dynamic_slice_in_dim(slope, first_head, share, 0)
    own_suffix, back_mem_tan = packed_scan((own_slope, slope_tan), CTX, True)
    back_mem = lax.all_gather(own_suffix, "probe", axis=0, tiled=True)

    mem_grad = jax.grad(memory_loss, argnums=(0, 2))
    (_, back_norm_inc), (query_curv, back_norm_inc_tan) = jax.jvp(
        lambda q, m, n: mem_grad(q, m, n, mem_weight),
        (query_rows, memory, normalizer),
        (query_dir, memory_tan, normalizer_tan),
    )
    back_norms = reduced_scan(jnp.concatenate((back_norm_inc, back_norm_inc_tan), axis=0), CTX, True)
    back_norm, back_norm_tan = back_norms[:heads], back_norms[heads:]

    through = jnp.einsum("shb,hab->sha", value_rows, back_mem, precision=HIGH) + back_norm[None]
    through_tan = (
        jnp.einsum("shb,hab->sha", value_dir, back_mem, precision=HIGH)
        + jnp.einsum("shb,hab->sha", value_rows, back_mem_tan, precision=HIGH)
        + back_norm_tan[None]
    )
    query_out = local_curv[0] + query_curv
    key_out = local_curv[1] + feature_curve(key_rows) * key_dir * through + key_slope * through_tan
    value_out = (
        local_curv[2]
        + jnp.einsum("sha,hab->shb", key_tan, back_mem, precision=HIGH)
        + jnp.einsum("sha,hab->shb", key_feat, back_mem_tan, precision=HIGH)
    )
    stacked = jnp.stack((query_out, key_out, value_out))
    products = stacked.reshape(1, 3, seg_rows, heads * head_size)
    partial_trace = jnp.sum(signs * stacked, axis=(1, 3)) / (seg_rows * groups)
    block_trace = lax.psum(partial_trace, "probe")
    return (products, block_trace.reshape(1, 3, heads))


def solution(mesh):
    ctx = mesh.shape["ctx"]
    inner = 4 if ctx % 4 == 0 else ctx
    devices = mesh.devices.reshape(ctx // inner, inner, mesh.shape["probe"])
    split = jax.sharding.Mesh(devices, ("outer", "inner", "probe"))
    placed = (P(None, CTX, None), P(CTX, None), P(), P("probe", None, CTX, None))
    return jax.shard_map(
        shards,
        mesh=split,
        in_specs=placed,
        out_specs=(P("probe", None, CTX, None), P(CTX, None, None)),
        check_vma=False,
    )
```

```python
import jax
import jax.numpy as jnp
from jax import lax
from jax.sharding import PartitionSpec as P

HIGH = lax.Precision.HIGH
CTX = ("outer", "inner")


def exclusive(block, reverse):
    count = block.shape[0]
    here = lax.broadcasted_iota(jnp.int32, (count, count), 0)
    there = lax.broadcasted_iota(jnp.int32, (count, count), 1)
    mask = (there > here) if reverse else (there < here)
    flat = block.reshape(count, -1)
    summed = jnp.dot(mask.astype(jnp.float32), flat, precision=lax.Precision.HIGHEST)
    return summed.reshape(block.shape)


def outer_exclusive(total, axis, reverse):
    count = lax.axis_size(axis)
    step = -1 if reverse else 1

    def shifted(value, by):
        pairs = [(i, i + step * by) for i in range(count) if 0 <= i + step * by < count]
        return lax.ppermute(value, axis, pairs)

    if count == 1:
        return jnp.zeros_like(total)
    acc = shifted(total, 1)
    by = 1
    while by < count - 1:
        acc = acc + shifted(acc, by)
        by *= 2
    return acc


def packed_scan(parts, axis, reverse):
    outer, inner = axis
    count = lax.axis_size(inner)
    width = parts[0].shape[-1]
    rows = [p.reshape(-1, width) for p in parts]
    sizes = [r.shape[0] for r in rows]
    total = sum(sizes)
    unit = 8 * count
    padded = -(-total // unit) * unit
    if padded > total:
        rows.append(jnp.zeros((padded - total, width), jnp.float32))
    buffer = jnp.concatenate(rows, axis=0).reshape(count, padded // count, width)
    spread = lax.all_to_all(buffer, inner, 0, 0)
    carry = outer_exclusive(jnp.sum(spread, axis=0), outer, reverse)
    scanned = exclusive(spread, reverse) + carry[None]
    back = lax.all_to_all(scanned, inner, 0, 0).reshape(padded, width)
    outs, row = [], 0
    for p, size in zip(parts, sizes):
        outs.append(back[row:row + size].reshape(p.shape))
        row += size
    return outs


def reduced_scan(part, axis, reverse):
    count = lax.axis_size(axis)
    place = lax.axis_index(axis)
    slot = lax.broadcasted_iota(jnp.int32, (count,) + (1,) * part.ndim, 0)
    every = lax.all_to_all(jnp.broadcast_to(part[None], (count,) + part.shape), axis, 0, 0)
    keep = (slot > place) if reverse else (slot < place)
    return jnp.sum(jnp.where(keep, every, 0.0), axis=0)


def feature_map(inputs):
    return jnp.where(inputs > 0, inputs + 1.0, jnp.exp(jnp.minimum(inputs, 0.0)))


def feature_slope(inputs):
    return jnp.where(inputs > 0, 1.0, jnp.exp(jnp.minimum(inputs, 0.0)))


def feature_curve(inputs):
    return jnp.where(inputs > 0, 0.0, jnp.exp(jnp.minimum(inputs, 0.0)))


def local_loss(query_rows, key_rows, value_rows, weight_rows):
    seg_rows = query_rows.shape[0]
    scale = query_rows.shape[-1] ** (-0.5)
    causal = lax.broadcasted_iota(jnp.int32, (seg_rows, seg_rows), 0) >= lax.broadcasted_iota(
        jnp.int32, (seg_rows, seg_rows), 1
    )
    logits = jnp.einsum("sha,tha->hst", query_rows, key_rows, precision=HIGH) * scale
    logits = jnp.where(causal[None], logits, -1e30)
    top = lax.stop_gradient(jnp.max(logits, axis=2, keepdims=True))
    weights = jnp.exp(logits - top)
    local_num = jnp.einsum("hst,thb->shb", weights, value_rows, precision=HIGH)
    local_den = jnp.transpose(jnp.sum(weights, axis=2))
    from_local = local_num / local_den[:, :, None]
    return jnp.sum(weight_rows * from_local)


def memory_loss(query_rows, memory, normalizer, weight_rows):
    query_feat = feature_map(query_rows)
    retrieved = jnp.einsum("sha,hab->shb", query_feat, memory, precision=HIGH)
    denom_mem = jnp.einsum("sha,ha->sh", query_feat, normalizer, precision=HIGH) + 1.0
    return jnp.sum(weight_rows * retrieved / denom_mem[:, :, None])


def memory_slope(query_rows, normalizer, weight_rows):
    query_feat = feature_map(query_rows)
    denom_mem = jnp.einsum("sha,ha->sh", query_feat, normalizer, precision=HIGH) + 1.0
    return jnp.einsum("sha,shb->hab", query_feat, weight_rows / denom_mem[:, :, None], precision=HIGH)


def shards(features, cotangent, gate_logits, probes):
    heads = gate_logits.shape[0]
    seg_rows = features.shape[1]
    head_size = features.shape[2] // heads
    shaped = features.reshape(3, seg_rows, heads, head_size)
    query_rows, key_rows, value_rows = (shaped[0], shaped[1], shaped[2])
    cot_rows = cotangent.reshape(seg_rows, heads, head_size)
    mixing = jax.nn.sigmoid(gate_logits)[None, :, None]
    mem_weight = cot_rows * mixing
    loc_weight = cot_rows * (1.0 - mixing)
    signs = probes[0].astype(jnp.float32).reshape(3, seg_rows, heads, head_size)
    query_dir, key_dir, value_dir = (signs[0], signs[1], signs[2])
    key_feat = feature_map(key_rows)
    key_slope = feature_slope(key_rows)
    key_tan = key_slope * key_dir
    groups = lax.axis_size("probe")
    share = heads // groups
    first_head = lax.axis_index("probe") * share

    local_grad = jax.grad(local_loss, argnums=(0, 1, 2))
    _, local_curv = jax.jvp(
        lambda q, k, v: local_grad(q, k, v, loc_weight),
        (query_rows, key_rows, value_rows),
        (query_dir, key_dir, value_dir),
    )

    increment = jnp.einsum("sha,shb->hab", key_feat, value_rows, precision=HIGH)
    increment_tan = jnp.einsum("sha,shb->hab", key_tan, value_rows, precision=HIGH) + jnp.einsum(
        "sha,shb->hab", key_feat, value_dir, precision=HIGH
    )
    norm_inc = jnp.sum(key_feat, axis=0)
    norm_tan = jnp.sum(key_tan, axis=0)
    own_inc = lax.dynamic_slice_in_dim(increment, first_head, share, 0)
    norms = reduced_scan(jnp.concatenate((norm_inc, norm_tan), axis=0), CTX, False)
    normalizer, normalizer_tan = norms[:heads], norms[heads:]
    own_prefix, memory_tan = packed_scan((own_inc, increment_tan), CTX, False)
    memory = lax.all_gather(own_prefix, "probe", axis=0, tiled=True)

    slope, slope_tan = jax.jvp(
        lambda q, n: memory_slope(q, n, mem_weight), (query_rows, normalizer), (query_dir, normalizer_tan)
    )
    own_slope = lax.dynamic_slice_in_dim(slope, first_head, share, 0)
    own_suffix, back_mem_tan = packed_scan((own_slope, slope_tan), CTX, True)
    back_mem = lax.all_gather(own_suffix, "probe", axis=0, tiled=True)

    mem_grad = jax.grad(memory_loss, argnums=(0, 2))
    (_, back_norm_inc), (query_curv, back_norm_inc_tan) = jax.jvp(
        lambda q, m, n: mem_grad(q, m, n, mem_weight),
        (query_rows, memory, normalizer),
        (query_dir, memory_tan, normalizer_tan),
    )
    back_norms = reduced_scan(jnp.concatenate((back_norm_inc, back_norm_inc_tan), axis=0), CTX, True)
    back_norm, back_norm_tan = back_norms[:heads], back_norms[heads:]

    through = jnp.einsum("shb,hab->sha", value_rows, back_mem, precision=HIGH) + back_norm[None]
    through_tan = (
        jnp.einsum("shb,hab->sha", value_dir, back_mem, precision=HIGH)
        + jnp.einsum("shb,hab->sha", value_rows, back_mem_tan, precision=HIGH)
        + back_norm_tan[None]
    )
    query_out = local_curv[0] + query_curv
    key_out = local_curv[1] + feature_curve(key_rows) * key_dir * through + key_slope * through_tan
    value_out = (
        local_curv[2]
        + jnp.einsum("sha,hab->shb", key_tan, back_mem, precision=HIGH)
        + jnp.einsum("sha,hab->shb", key_feat, back_mem_tan, precision=HIGH)
    )
    stacked = jnp.stack((query_out, key_out, value_out))
    products = stacked.reshape(1, 3, seg_rows, heads * head_size)
    partial_trace = jnp.sum(signs * stacked, axis=(1, 3)) / (seg_rows * groups)
    block_trace = lax.psum(partial_trace, "probe")
    return (products, block_trace.reshape(1, 3, heads))


def solution(mesh):
    ctx = mesh.shape["ctx"]
    inner = 4 if ctx % 4 == 0 else ctx
    devices = mesh.devices.reshape(ctx // inner, inner, mesh.shape["probe"])
    split = jax.sharding.Mesh(devices, ("outer", "inner", "probe"))
    placed = (P(None, CTX, None), P(CTX, None), P(), P("probe", None, CTX, None))
    return jax.shard_map(
        shards,
        mesh=split,
        in_specs=placed,
        out_specs=(P("probe", None, CTX, None), P(CTX, None, None)),
        check_vma=False,
    )
```

```python
import jax
import jax.numpy as jnp
from jax import lax
from jax.sharding import PartitionSpec as P

HIGH = lax.Precision.HIGH
CTX = ("outer", "inner")


def exclusive(block, reverse):
    count = block.shape[0]
    here = lax.broadcasted_iota(jnp.int32, (count, count), 0)
    there = lax.broadcasted_iota(jnp.int32, (count, count), 1)
    mask = (there > here) if reverse else (there < here)
    flat = block.reshape(count, -1)
    summed = jnp.dot(mask.astype(jnp.float32), flat, precision=lax.Precision.HIGHEST)
    return summed.reshape(block.shape)


def outer_exclusive(total, axis, reverse):
    count = lax.axis_size(axis)
    step = -1 if reverse else 1

    def shifted(value, by):
        pairs = [(i, i + step * by) for i in range(count) if 0 <= i + step * by < count]
        return lax.ppermute(value, axis, pairs)

    if count == 1:
        return jnp.zeros_like(total)
    acc = shifted(total, 1)
    by = 1
    while by < count - 1:
        acc = acc + shifted(acc, by)
        by *= 2
    return acc


def packed_scan(parts, axis, reverse, tie=None):
    outer, inner = axis
    count = lax.axis_size(inner)
    width = parts[0].shape[-1]
    rows = [p.reshape(-1, width) for p in parts]
    sizes = [r.shape[0] for r in rows]
    total = sum(sizes)
    unit = 8 * count
    padded = -(-total // unit) * unit
    if padded > total:
        rows.append(jnp.zeros((padded - total, width), jnp.float32))
    buffer = jnp.concatenate(rows, axis=0).reshape(count, padded // count, width)
    spread = lax.all_to_all(buffer, inner, 0, 0)
    carry = outer_exclusive(jnp.sum(spread, axis=0), outer, reverse)
    scanned = exclusive(spread, reverse) + carry[None]
    if tie is not None:
        scanned, tie = lax.optimization_barrier((scanned, tie))
    back = lax.all_to_all(scanned, inner, 0, 0).reshape(padded, width)
    outs, row = [], 0
    for p, size in zip(parts, sizes):
        outs.append(back[row:row + size].reshape(p.shape))
        row += size
    return outs, tie


def reduced_scan(part, axis, reverse):
    count = lax.axis_size(axis)
    place = lax.axis_index(axis)
    slot = lax.broadcasted_iota(jnp.int32, (count,) + (1,) * part.ndim, 0)
    every = lax.all_to_all(jnp.broadcast_to(part[None], (count,) + part.shape), axis, 0, 0)
    keep = (slot > place) if reverse else (slot < place)
    return jnp.sum(jnp.where(keep, every, 0.0), axis=0)


def feature_map(inputs):
    return jnp.where(inputs > 0, inputs + 1.0, jnp.exp(jnp.minimum(inputs, 0.0)))


def feature_slope(inputs):
    return jnp.where(inputs > 0, 1.0, jnp.exp(jnp.minimum(inputs, 0.0)))


def feature_curve(inputs):
    return jnp.where(inputs > 0, 0.0, jnp.exp(jnp.minimum(inputs, 0.0)))


def local_loss(query_rows, key_rows, value_rows, weight_rows):
    seg_rows = query_rows.shape[0]
    scale = query_rows.shape[-1] ** (-0.5)
    causal = lax.broadcasted_iota(jnp.int32, (seg_rows, seg_rows), 0) >= lax.broadcasted_iota(
        jnp.int32, (seg_rows, seg_rows), 1
    )
    logits = jnp.einsum("sha,tha->hst", query_rows, key_rows, precision=HIGH) * scale
    logits = jnp.where(causal[None], logits, -1e30)
    top = lax.stop_gradient(jnp.max(logits, axis=2, keepdims=True))
    weights = jnp.exp(logits - top)
    local_num = jnp.einsum("hst,thb->shb", weights, value_rows, precision=HIGH)
    local_den = jnp.transpose(jnp.sum(weights, axis=2))
    from_local = local_num / local_den[:, :, None]
    return jnp.sum(weight_rows * from_local)


def memory_loss(query_rows, memory, normalizer, weight_rows):
    query_feat = feature_map(query_rows)
    retrieved = jnp.einsum("sha,hab->shb", query_feat, memory, precision=HIGH)
    denom_mem = jnp.einsum("sha,ha->sh", query_feat, normalizer, precision=HIGH) + 1.0
    return jnp.sum(weight_rows * retrieved / denom_mem[:, :, None])


def memory_slope(query_rows, normalizer, weight_rows):
    query_feat = feature_map(query_rows)
    denom_mem = jnp.einsum("sha,ha->sh", query_feat, normalizer, precision=HIGH) + 1.0
    return jnp.einsum("sha,shb->hab", query_feat, weight_rows / denom_mem[:, :, None], precision=HIGH)


def shards(features, cotangent, gate_logits, probes):
    heads = gate_logits.shape[0]
    seg_rows = features.shape[1]
    head_size = features.shape[2] // heads
    shaped = features.reshape(3, seg_rows, heads, head_size)
    query_rows, key_rows, value_rows = (shaped[0], shaped[1], shaped[2])
    cot_rows = cotangent.reshape(seg_rows, heads, head_size)
    mixing = jax.nn.sigmoid(gate_logits)[None, :, None]
    mem_weight = cot_rows * mixing
    loc_weight = cot_rows * (1.0 - mixing)
    signs = probes[0].astype(jnp.float32).reshape(3, seg_rows, heads, head_size)
    query_dir, key_dir, value_dir = (signs[0], signs[1], signs[2])
    key_feat = feature_map(key_rows)
    key_slope = feature_slope(key_rows)
    key_tan = key_slope * key_dir
    groups = lax.axis_size("probe")
    share = heads // groups
    first_head = lax.axis_index("probe") * share

    local_grad = jax.grad(local_loss, argnums=(0, 1, 2))
    _, local_curv = jax.jvp(
        lambda q, k, v: local_grad(q, k, v, loc_weight),
        (query_rows, key_rows, value_rows),
        (query_dir, key_dir, value_dir),
    )

    increment = jnp.einsum("sha,shb->hab", key_feat, value_rows, precision=HIGH)
    increment_tan = jnp.einsum("sha,shb->hab", key_tan, value_rows, precision=HIGH) + jnp.einsum(
        "sha,shb->hab", key_feat, value_dir, precision=HIGH
    )
    norm_inc = jnp.sum(key_feat, axis=0)
    norm_tan = jnp.sum(key_tan, axis=0)
    own_inc = lax.dynamic_slice_in_dim(increment, first_head, share, 0)
    norms = reduced_scan(jnp.concatenate((norm_inc, norm_tan), axis=0), CTX, False)
    normalizer, normalizer_tan = norms[:heads], norms[heads:]
    (own_prefix, memory_tan), _ = packed_scan((own_inc, increment_tan), CTX, False)
    memory = lax.all_gather(own_prefix, "probe", axis=0, tiled=True)

    slope, slope_tan = jax.jvp(
        lambda q, n: memory_slope(q, n, mem_weight), (query_rows, normalizer), (query_dir, normalizer_tan)
    )
    mem_grad = jax.grad(memory_loss, argnums=(0, 2))
    (_, back_norm_inc), (query_curv, back_norm_inc_tan) = jax.jvp(
        lambda q, m, n: mem_grad(q, m, n, mem_weight),
        (query_rows, memory, normalizer),
        (query_dir, memory_tan, normalizer_tan),
    )
    back_norms = reduced_scan(jnp.concatenate((back_norm_inc, back_norm_inc_tan), axis=0), CTX, True)
    own_slope = lax.dynamic_slice_in_dim(slope, first_head, share, 0)
    (own_suffix, back_mem_tan), back_norms = packed_scan((own_slope, slope_tan), CTX, True, back_norms)
    back_norm, back_norm_tan = back_norms[:heads], back_norms[heads:]
    back_mem = lax.all_gather(own_suffix, "probe", axis=0, tiled=True)

    through = jnp.einsum("shb,hab->sha", value_rows, back_mem, precision=HIGH) + back_norm[None]
    through_tan = (
        jnp.einsum("shb,hab->sha", value_dir, back_mem, precision=HIGH)
        + jnp.einsum("shb,hab->sha", value_rows, back_mem_tan, precision=HIGH)
        + back_norm_tan[None]
    )
    query_out = local_curv[0] + query_curv
    key_out = local_curv[1] + feature_curve(key_rows) * key_dir * through + key_slope * through_tan
    value_out = (
        local_curv[2]
        + jnp.einsum("sha,hab->shb", key_tan, back_mem, precision=HIGH)
        + jnp.einsum("sha,hab->shb", key_feat, back_mem_tan, precision=HIGH)
    )
    stacked = jnp.stack((query_out, key_out, value_out))
    products = stacked.reshape(1, 3, seg_rows, heads * head_size)
    partial_trace = jnp.sum(signs * stacked, axis=(1, 3)) / (seg_rows * groups)
    block_trace = lax.psum(partial_trace, "probe")
    return (products, block_trace.reshape(1, 3, heads))


def solution(mesh):
    ctx = mesh.shape["ctx"]
    inner = 4 if ctx % 4 == 0 else ctx
    devices = mesh.devices.reshape(ctx // inner, inner, mesh.shape["probe"])
    split = jax.sharding.Mesh(devices, ("outer", "inner", "probe"))
    placed = (P(None, CTX, None), P(CTX, None), P(), P("probe", None, CTX, None))
    return jax.shard_map(
        shards,
        mesh=split,
        in_specs=placed,
        out_specs=(P("probe", None, CTX, None), P(CTX, None, None)),
        check_vma=False,
    )
```

```python
import jax
import jax.numpy as jnp
from jax import lax
from jax.sharding import PartitionSpec as P

HIGH = lax.Precision.HIGH
CTX = ("outer", "inner")


def exclusive(block, reverse):
    count = block.shape[0]
    here = lax.broadcasted_iota(jnp.int32, (count, count), 0)
    there = lax.broadcasted_iota(jnp.int32, (count, count), 1)
    mask = (there > here) if reverse else (there < here)
    flat = block.reshape(count, -1)
    summed = jnp.dot(mask.astype(jnp.float32), flat, precision=lax.Precision.HIGHEST)
    return summed.reshape(block.shape)


def outer_exclusive(total, axis, reverse):
    count = lax.axis_size(axis)
    step = -1 if reverse else 1

    def shifted(value, by):
        pairs = [(i, i + step * by) for i in range(count) if 0 <= i + step * by < count]
        return lax.ppermute(value, axis, pairs)

    if count == 1:
        return jnp.zeros_like(total)
    acc = shifted(total, 1)
    by = 1
    while by < count - 1:
        acc = acc + shifted(acc, by)
        by *= 2
    return acc


def scan_open(parts, axis, reverse):
    outer, inner = axis
    count = lax.axis_size(inner)
    width = parts[0].shape[-1]
    rows = [p.reshape(-1, width) for p in parts]
    sizes = [r.shape[0] for r in rows]
    total = sum(sizes)
    unit = 8 * count
    padded = -(-total // unit) * unit
    if padded > total:
        rows.append(jnp.zeros((padded - total, width), jnp.float32))
    buffer = jnp.concatenate(rows, axis=0).reshape(count, padded // count, width)
    spread = lax.all_to_all(buffer, inner, 0, 0)
    carry = outer_exclusive(jnp.sum(spread, axis=0), outer, reverse)
    return exclusive(spread, reverse) + carry[None], (parts, sizes, padded, width)


def scan_close(scanned, layout, axis):
    parts, sizes, padded, width = layout
    back = lax.all_to_all(scanned, axis[1], 0, 0).reshape(padded, width)
    outs, row = [], 0
    for p, size in zip(parts, sizes):
        outs.append(back[row:row + size].reshape(p.shape))
        row += size
    return outs


def reduced_scan(part, axis, reverse):
    count = lax.axis_size(axis)
    place = lax.axis_index(axis)
    slot = lax.broadcasted_iota(jnp.int32, (count,) + (1,) * part.ndim, 0)
    every = lax.all_to_all(jnp.broadcast_to(part[None], (count,) + part.shape), axis, 0, 0)
    keep = (slot > place) if reverse else (slot < place)
    return jnp.sum(jnp.where(keep, every, 0.0), axis=0)


def feature_map(inputs):
    return jnp.where(inputs > 0, inputs + 1.0, jnp.exp(jnp.minimum(inputs, 0.0)))


def feature_slope(inputs):
    return jnp.where(inputs > 0, 1.0, jnp.exp(jnp.minimum(inputs, 0.0)))


def feature_curve(inputs):
    return jnp.where(inputs > 0, 0.0, jnp.exp(jnp.minimum(inputs, 0.0)))


def local_loss(query_rows, key_rows, value_rows, weight_rows):
    seg_rows = query_rows.shape[0]
    scale = query_rows.shape[-1] ** (-0.5)
    causal = lax.broadcasted_iota(jnp.int32, (seg_rows, seg_rows), 0) >= lax.broadcasted_iota(
        jnp.int32, (seg_rows, seg_rows), 1
    )
    logits = jnp.einsum("sha,tha->hst", query_rows, key_rows, precision=HIGH) * scale
    logits = jnp.where(causal[None], logits, -1e30)
    top = lax.stop_gradient(jnp.max(logits, axis=2, keepdims=True))
    weights = jnp.exp(logits - top)
    local_num = jnp.einsum("hst,thb->shb", weights, value_rows, precision=HIGH)
    local_den = jnp.transpose(jnp.sum(weights, axis=2))
    from_local = local_num / local_den[:, :, None]
    return jnp.sum(weight_rows * from_local)


def memory_loss(query_rows, memory, normalizer, weight_rows):
    query_feat = feature_map(query_rows)
    retrieved = jnp.einsum("sha,hab->shb", query_feat, memory, precision=HIGH)
    denom_mem = jnp.einsum("sha,ha->sh", query_feat, normalizer, precision=HIGH) + 1.0
    return jnp.sum(weight_rows * retrieved / denom_mem[:, :, None])


def memory_slope(query_rows, normalizer, weight_rows):
    query_feat = feature_map(query_rows)
    denom_mem = jnp.einsum("sha,ha->sh", query_feat, normalizer, precision=HIGH) + 1.0
    return jnp.einsum("sha,shb->hab", query_feat, weight_rows / denom_mem[:, :, None], precision=HIGH)


def shards(features, cotangent, gate_logits, probes):
    heads = gate_logits.shape[0]
    seg_rows = features.shape[1]
    head_size = features.shape[2] // heads
    shaped = features.reshape(3, seg_rows, heads, head_size)
    query_rows, key_rows, value_rows = (shaped[0], shaped[1], shaped[2])
    cot_rows = cotangent.reshape(seg_rows, heads, head_size)
    mixing = jax.nn.sigmoid(gate_logits)[None, :, None]
    mem_weight = cot_rows * mixing
    loc_weight = cot_rows * (1.0 - mixing)
    signs = probes[0].astype(jnp.float32).reshape(3, seg_rows, heads, head_size)
    query_dir, key_dir, value_dir = (signs[0], signs[1], signs[2])
    key_feat = feature_map(key_rows)
    key_slope = feature_slope(key_rows)
    key_tan = key_slope * key_dir
    groups = lax.axis_size("probe")
    share = heads // groups
    first_head = lax.axis_index("probe") * share

    local_grad = jax.grad(local_loss, argnums=(0, 1, 2))
    _, local_curv = jax.jvp(
        lambda q, k, v: local_grad(q, k, v, loc_weight),
        (query_rows, key_rows, value_rows),
        (query_dir, key_dir, value_dir),
    )

    increment = jnp.einsum("sha,shb->hab", key_feat, value_rows, precision=HIGH)
    increment_tan = jnp.einsum("sha,shb->hab", key_tan, value_rows, precision=HIGH) + jnp.einsum(
        "sha,shb->hab", key_feat, value_dir, precision=HIGH
    )
    norm_inc = jnp.sum(key_feat, axis=0)
    norm_tan = jnp.sum(key_tan, axis=0)
    own_inc = lax.dynamic_slice_in_dim(increment, first_head, share, 0)
    norms = reduced_scan(jnp.concatenate((norm_inc, norm_tan), axis=0), CTX, False)
    normalizer, normalizer_tan = norms[:heads], norms[heads:]
    forward_open, forward_layout = scan_open((own_inc, increment_tan), CTX, False)

    slope, slope_tan = jax.jvp(
        lambda q, n: memory_slope(q, n, mem_weight), (query_rows, normalizer), (query_dir, normalizer_tan)
    )
    own_slope = lax.dynamic_slice_in_dim(slope, first_head, share, 0)
    backward_open, backward_layout = scan_open((own_slope, slope_tan), CTX, True)
    forward_open, backward_open = lax.optimization_barrier((forward_open, backward_open))
    own_prefix, memory_tan = scan_close(forward_open, forward_layout, CTX)
    memory = lax.all_gather(own_prefix, "probe", axis=0, tiled=True)
    own_suffix, back_mem_tan = scan_close(backward_open, backward_layout, CTX)
    back_mem = lax.all_gather(own_suffix, "probe", axis=0, tiled=True)

    mem_grad = jax.grad(memory_loss, argnums=(0, 2))
    (_, back_norm_inc), (query_curv, back_norm_inc_tan) = jax.jvp(
        lambda q, m, n: mem_grad(q, m, n, mem_weight),
        (query_rows, memory, normalizer),
        (query_dir, memory_tan, normalizer_tan),
    )
    back_norms = reduced_scan(jnp.concatenate((back_norm_inc, back_norm_inc_tan), axis=0), CTX, True)
    back_norm, back_norm_tan = back_norms[:heads], back_norms[heads:]

    through = jnp.einsum("shb,hab->sha", value_rows, back_mem, precision=HIGH) + back_norm[None]
    through_tan = (
        jnp.einsum("shb,hab->sha", value_dir, back_mem, precision=HIGH)
        + jnp.einsum("shb,hab->sha", value_rows, back_mem_tan, precision=HIGH)
        + back_norm_tan[None]
    )
    query_out = local_curv[0] + query_curv
    key_out = local_curv[1] + feature_curve(key_rows) * key_dir * through + key_slope * through_tan
    value_out = (
        local_curv[2]
        + jnp.einsum("sha,hab->shb", key_tan, back_mem, precision=HIGH)
        + jnp.einsum("sha,hab->shb", key_feat, back_mem_tan, precision=HIGH)
    )
    stacked = jnp.stack((query_out, key_out, value_out))
    products = stacked.reshape(1, 3, seg_rows, heads * head_size)
    partial_trace = jnp.sum(signs * stacked, axis=(1, 3)) / (seg_rows * groups)
    block_trace = lax.psum(partial_trace, "probe")
    return (products, block_trace.reshape(1, 3, heads))


def solution(mesh):
    ctx = mesh.shape["ctx"]
    inner = 4 if ctx % 4 == 0 else ctx
    devices = mesh.devices.reshape(ctx // inner, inner, mesh.shape["probe"])
    split = jax.sharding.Mesh(devices, ("outer", "inner", "probe"))
    placed = (P(None, CTX, None), P(CTX, None), P(), P("probe", None, CTX, None))
    return jax.shard_map(
        shards,
        mesh=split,
        in_specs=placed,
        out_specs=(P("probe", None, CTX, None), P(CTX, None, None)),
        check_vma=False,
    )
```

```python
import jax
import jax.numpy as jnp
from jax import lax
from jax.sharding import PartitionSpec as P

HIGH = lax.Precision.HIGH
CTX = ("outer", "inner")


def exclusive(block, reverse):
    count = block.shape[0]
    order = list(range(count - 1, -1, -1)) if reverse else list(range(count))
    sums = [None] * count
    running = jnp.zeros_like(block[0])
    for index in order:
        sums[index] = running
        running = running + block[index]
    return jnp.stack(sums)


def outer_exclusive(total, axis, reverse):
    count = lax.axis_size(axis)
    step = -1 if reverse else 1

    def shifted(value, by):
        pairs = [(i, i + step * by) for i in range(count) if 0 <= i + step * by < count]
        return lax.ppermute(value, axis, pairs)

    if count == 1:
        return jnp.zeros_like(total)
    acc = shifted(total, 1)
    by = 1
    while by < count - 1:
        acc = acc + shifted(acc, by)
        by *= 2
    return acc


def scan_open(parts, axis, reverse):
    outer, inner = axis
    count = lax.axis_size(inner)
    width = parts[0].shape[-1]
    rows = [p.reshape(-1, width) for p in parts]
    sizes = [r.shape[0] for r in rows]
    total = sum(sizes)
    unit = 8 * count
    padded = -(-total // unit) * unit
    if padded > total:
        rows.append(jnp.zeros((padded - total, width), jnp.float32))
    buffer = jnp.concatenate(rows, axis=0).reshape(count, padded // count, width)
    spread = lax.all_to_all(buffer, inner, 0, 0)
    carry = outer_exclusive(jnp.sum(spread, axis=0), outer, reverse)
    return exclusive(spread, reverse) + carry[None], (parts, sizes, padded, width)


def scan_close(scanned, layout, axis):
    parts, sizes, padded, width = layout
    back = lax.all_to_all(scanned, axis[1], 0, 0).reshape(padded, width)
    outs, row = [], 0
    for p, size in zip(parts, sizes):
        outs.append(back[row:row + size].reshape(p.shape))
        row += size
    return outs


def reduced_scan(part, axis, reverse):
    count = lax.axis_size(axis)
    place = lax.axis_index(axis)
    slot = lax.broadcasted_iota(jnp.int32, (count,) + (1,) * part.ndim, 0)
    every = lax.all_to_all(jnp.broadcast_to(part[None], (count,) + part.shape), axis, 0, 0)
    keep = (slot > place) if reverse else (slot < place)
    return jnp.sum(jnp.where(keep, every, 0.0), axis=0)


def feature_map(inputs):
    return jnp.where(inputs > 0, inputs + 1.0, jnp.exp(jnp.minimum(inputs, 0.0)))


def feature_slope(inputs):
    return jnp.where(inputs > 0, 1.0, jnp.exp(jnp.minimum(inputs, 0.0)))


def feature_curve(inputs):
    return jnp.where(inputs > 0, 0.0, jnp.exp(jnp.minimum(inputs, 0.0)))


def local_loss(query_rows, key_rows, value_rows, weight_rows):
    seg_rows = query_rows.shape[0]
    scale = query_rows.shape[-1] ** (-0.5)
    causal = lax.broadcasted_iota(jnp.int32, (seg_rows, seg_rows), 0) >= lax.broadcasted_iota(
        jnp.int32, (seg_rows, seg_rows), 1
    )
    logits = jnp.einsum("sha,tha->hst", query_rows, key_rows, precision=HIGH) * scale
    logits = jnp.where(causal[None], logits, -1e30)
    top = lax.stop_gradient(jnp.max(logits, axis=2, keepdims=True))
    weights = jnp.exp(logits - top)
    local_num = jnp.einsum("hst,thb->shb", weights, value_rows, precision=HIGH)
    local_den = jnp.transpose(jnp.sum(weights, axis=2))
    from_local = local_num / local_den[:, :, None]
    return jnp.sum(weight_rows * from_local)


def memory_loss(query_rows, memory, normalizer, weight_rows):
    query_feat = feature_map(query_rows)
    retrieved = jnp.einsum("sha,hab->shb", query_feat, memory, precision=HIGH)
    denom_mem = jnp.einsum("sha,ha->sh", query_feat, normalizer, precision=HIGH) + 1.0
    return jnp.sum(weight_rows * retrieved / denom_mem[:, :, None])


def memory_slope(query_rows, normalizer, weight_rows):
    query_feat = feature_map(query_rows)
    denom_mem = jnp.einsum("sha,ha->sh", query_feat, normalizer, precision=HIGH) + 1.0
    return jnp.einsum("sha,shb->hab", query_feat, weight_rows / denom_mem[:, :, None], precision=HIGH)


def shards(features, cotangent, gate_logits, probes):
    heads = gate_logits.shape[0]
    seg_rows = features.shape[1]
    head_size = features.shape[2] // heads
    shaped = features.reshape(3, seg_rows, heads, head_size)
    query_rows, key_rows, value_rows = (shaped[0], shaped[1], shaped[2])
    cot_rows = cotangent.reshape(seg_rows, heads, head_size)
    mixing = jax.nn.sigmoid(gate_logits)[None, :, None]
    mem_weight = cot_rows * mixing
    loc_weight = cot_rows * (1.0 - mixing)
    signs = probes[0].astype(jnp.float32).reshape(3, seg_rows, heads, head_size)
    query_dir, key_dir, value_dir = (signs[0], signs[1], signs[2])
    key_feat = feature_map(key_rows)
    key_slope = feature_slope(key_rows)
    key_tan = key_slope * key_dir
    groups = lax.axis_size("probe")
    share = heads // groups
    first_head = lax.axis_index("probe") * share

    local_grad = jax.grad(local_loss, argnums=(0, 1, 2))
    _, local_curv = jax.jvp(
        lambda q, k, v: local_grad(q, k, v, loc_weight),
        (query_rows, key_rows, value_rows),
        (query_dir, key_dir, value_dir),
    )

    increment = jnp.einsum("sha,shb->hab", key_feat, value_rows, precision=HIGH)
    increment_tan = jnp.einsum("sha,shb->hab", key_tan, value_rows, precision=HIGH) + jnp.einsum(
        "sha,shb->hab", key_feat, value_dir, precision=HIGH
    )
    norm_inc = jnp.sum(key_feat, axis=0)
    norm_tan = jnp.sum(key_tan, axis=0)
    own_inc = lax.dynamic_slice_in_dim(increment, first_head, share, 0)
    norms = reduced_scan(jnp.concatenate((norm_inc, norm_tan), axis=0), CTX, False)
    normalizer, normalizer_tan = norms[:heads], norms[heads:]
    forward_open, forward_layout = scan_open((own_inc, increment_tan), CTX, False)

    slope, slope_tan = jax.jvp(
        lambda q, n: memory_slope(q, n, mem_weight), (query_rows, normalizer), (query_dir, normalizer_tan)
    )
    own_slope = lax.dynamic_slice_in_dim(slope, first_head, share, 0)
    backward_open, backward_layout = scan_open((own_slope, slope_tan), CTX, True)
    forward_open, backward_open = lax.optimization_barrier((forward_open, backward_open))
    own_prefix, memory_tan = scan_close(forward_open, forward_layout, CTX)
    memory = lax.all_gather(own_prefix, "probe", axis=0, tiled=True)
    own_suffix, back_mem_tan = scan_close(backward_open, backward_layout, CTX)
    back_mem = lax.all_gather(own_suffix, "probe", axis=0, tiled=True)

    mem_grad = jax.grad(memory_loss, argnums=(0, 2))
    (_, back_norm_inc), (query_curv, back_norm_inc_tan) = jax.jvp(
        lambda q, m, n: mem_grad(q, m, n, mem_weight),
        (query_rows, memory, normalizer),
        (query_dir, memory_tan, normalizer_tan),
    )
    back_norms = reduced_scan(jnp.concatenate((back_norm_inc, back_norm_inc_tan), axis=0), CTX, True)
    back_norm, back_norm_tan = back_norms[:heads], back_norms[heads:]

    through = jnp.einsum("shb,hab->sha", value_rows, back_mem, precision=HIGH) + back_norm[None]
    through_tan = (
        jnp.einsum("shb,hab->sha", value_dir, back_mem, precision=HIGH)
        + jnp.einsum("shb,hab->sha", value_rows, back_mem_tan, precision=HIGH)
        + back_norm_tan[None]
    )
    query_out = local_curv[0] + query_curv
    key_out = local_curv[1] + feature_curve(key_rows) * key_dir * through + key_slope * through_tan
    value_out = (
        local_curv[2]
        + jnp.einsum("sha,hab->shb", key_tan, back_mem, precision=HIGH)
        + jnp.einsum("sha,hab->shb", key_feat, back_mem_tan, precision=HIGH)
    )
    stacked = jnp.stack((query_out, key_out, value_out))
    products = stacked.reshape(1, 3, seg_rows, heads * head_size)
    partial_trace = jnp.sum(signs * stacked, axis=(1, 3)) / (seg_rows * groups)
    block_trace = lax.psum(partial_trace, "probe")
    return (products, block_trace.reshape(1, 3, heads))


def solution(mesh):
    ctx = mesh.shape["ctx"]
    inner = 4 if ctx % 4 == 0 else ctx
    devices = mesh.devices.reshape(ctx // inner, inner, mesh.shape["probe"])
    split = jax.sharding.Mesh(devices, ("outer", "inner", "probe"))
    placed = (P(None, CTX, None), P(CTX, None), P(), P("probe", None, CTX, None))
    return jax.shard_map(
        shards,
        mesh=split,
        in_specs=placed,
        out_specs=(P("probe", None, CTX, None), P(CTX, None, None)),
        check_vma=False,
    )
```

```python
import jax
import jax.numpy as jnp
from jax import lax
from jax.sharding import PartitionSpec as P

HIGH = lax.Precision.HIGH
CTX = ("outer", "inner")


def exclusive(block, reverse):
    count = block.shape[0]
    order = list(range(count - 1, -1, -1)) if reverse else list(range(count))
    sums = [None] * count
    running = jnp.zeros_like(block[0])
    for index in order:
        sums[index] = running
        running = running + block[index]
    return jnp.stack(sums)


def outer_exclusive(total, axis, reverse):
    count = lax.axis_size(axis)
    step = -1 if reverse else 1

    def shifted(value, by):
        pairs = [(i, i + step * by) for i in range(count) if 0 <= i + step * by < count]
        return lax.ppermute(value, axis, pairs)

    if count == 1:
        return jnp.zeros_like(total)
    acc = shifted(total, 1)
    by = 1
    while by < count - 1:
        acc = acc + shifted(acc, by)
        by *= 2
    return acc


def scan_open(parts, axis, reverse):
    outer, inner = axis
    count = lax.axis_size(inner)
    width = parts[0].shape[-1]
    rows = [p.reshape(-1, width) for p in parts]
    sizes = [r.shape[0] for r in rows]
    total = sum(sizes)
    unit = 8 * count
    padded = -(-total // unit) * unit
    if padded > total:
        rows.append(jnp.zeros((padded - total, width), jnp.float32))
    buffer = jnp.concatenate(rows, axis=0).reshape(count, padded // count, width)
    spread = lax.all_to_all(buffer, inner, 0, 0)
    carry = outer_exclusive(jnp.sum(spread, axis=0), outer, reverse)
    return exclusive(spread, reverse) + carry[None], (parts, sizes, padded, width)


def scan_close(scanned, layout, axis):
    parts, sizes, padded, width = layout
    back = lax.all_to_all(scanned, axis[1], 0, 0).reshape(padded, width)
    outs, row = [], 0
    for p, size in zip(parts, sizes):
        outs.append(back[row:row + size].reshape(p.shape))
        row += size
    return outs


def reduced_scan(part, axis, reverse):
    count = lax.axis_size(axis)
    place = lax.axis_index(axis)
    slot = lax.broadcasted_iota(jnp.int32, (count,) + (1,) * part.ndim, 0)
    every = lax.all_to_all(jnp.broadcast_to(part[None], (count,) + part.shape), axis, 0, 0)
    keep = (slot > place) if reverse else (slot < place)
    return jnp.sum(jnp.where(keep, every, 0.0), axis=0)


def feature_map(inputs):
    return jnp.where(inputs > 0, inputs + 1.0, jnp.exp(jnp.minimum(inputs, 0.0)))


def feature_slope(inputs):
    return jnp.where(inputs > 0, 1.0, jnp.exp(jnp.minimum(inputs, 0.0)))


def feature_curve(inputs):
    return jnp.where(inputs > 0, 0.0, jnp.exp(jnp.minimum(inputs, 0.0)))


def local_loss(query_rows, key_rows, value_rows, weight_rows):
    seg_rows = query_rows.shape[0]
    scale = query_rows.shape[-1] ** (-0.5)
    causal = lax.broadcasted_iota(jnp.int32, (seg_rows, seg_rows), 0) >= lax.broadcasted_iota(
        jnp.int32, (seg_rows, seg_rows), 1
    )
    logits = jnp.einsum("sha,tha->hst", query_rows, key_rows, precision=HIGH) * scale
    logits = jnp.where(causal[None], logits, -1e30)
    top = lax.stop_gradient(jnp.max(logits, axis=2, keepdims=True))
    weights = jnp.exp(logits - top)
    local_num = jnp.einsum("hst,thb->shb", weights, value_rows, precision=HIGH)
    local_den = jnp.transpose(jnp.sum(weights, axis=2))
    from_local = local_num / local_den[:, :, None]
    return jnp.sum(weight_rows * from_local)


def memory_loss(query_rows, memory, normalizer, weight_rows):
    query_feat = feature_map(query_rows)
    retrieved = jnp.einsum("sha,hab->shb", query_feat, memory, precision=HIGH)
    denom_mem = jnp.einsum("sha,ha->sh", query_feat, normalizer, precision=HIGH) + 1.0
    return jnp.sum(weight_rows * retrieved / denom_mem[:, :, None])


def memory_slope(query_rows, normalizer, weight_rows):
    query_feat = feature_map(query_rows)
    denom_mem = jnp.einsum("sha,ha->sh", query_feat, normalizer, precision=HIGH) + 1.0
    return jnp.einsum("sha,shb->hab", query_feat, weight_rows / denom_mem[:, :, None], precision=HIGH)


def shards(features, cotangent, gate_logits, probes):
    heads = gate_logits.shape[0]
    seg_rows = features.shape[1]
    head_size = features.shape[2] // heads
    shaped = features.reshape(3, seg_rows, heads, head_size)
    query_rows, key_rows, value_rows = (shaped[0], shaped[1], shaped[2])
    cot_rows = cotangent.reshape(seg_rows, heads, head_size)
    mixing = jax.nn.sigmoid(gate_logits)[None, :, None]
    mem_weight = cot_rows * mixing
    loc_weight = cot_rows * (1.0 - mixing)
    signs = probes[0].astype(jnp.float32).reshape(3, seg_rows, heads, head_size)
    query_dir, key_dir, value_dir = (signs[0], signs[1], signs[2])
    key_feat = feature_map(key_rows)
    key_slope = feature_slope(key_rows)
    key_tan = key_slope * key_dir
    groups = lax.axis_size("probe")
    share = heads // groups
    first_head = lax.axis_index("probe") * share

    local_grad = jax.grad(local_loss, argnums=(0, 1, 2))
    _, local_curv = jax.jvp(
        lambda q, k, v: local_grad(q, k, v, loc_weight),
        (query_rows, key_rows, value_rows),
        (query_dir, key_dir, value_dir),
    )

    increment = jnp.einsum("sha,shb->hab", key_feat, value_rows, precision=HIGH)
    increment_tan = jnp.einsum("sha,shb->hab", key_tan, value_rows, precision=HIGH) + jnp.einsum(
        "sha,shb->hab", key_feat, value_dir, precision=HIGH
    )
    norm_inc = jnp.sum(key_feat, axis=0)
    norm_tan = jnp.sum(key_tan, axis=0)
    own_inc = lax.dynamic_slice_in_dim(increment, first_head, share, 0)
    norms = reduced_scan(jnp.concatenate((norm_inc, norm_tan), axis=0), CTX, False)
    normalizer, normalizer_tan = norms[:heads], norms[heads:]
    forward_open, forward_layout = scan_open((own_inc, increment_tan), CTX, False)

    slope, slope_tan = jax.jvp(
        lambda q, n: memory_slope(q, n, mem_weight), (query_rows, normalizer), (query_dir, normalizer_tan)
    )
    own_slope = lax.dynamic_slice_in_dim(slope, first_head, share, 0)
    backward_open, backward_layout = scan_open((own_slope, slope_tan), CTX, True)
    forward_open, backward_open = lax.optimization_barrier((forward_open, backward_open))
    own_prefix, memory_tan = scan_close(forward_open, forward_layout, CTX)
    memory = lax.all_gather(own_prefix, "probe", axis=0, tiled=True)
    mem_grad = jax.grad(memory_loss, argnums=(0, 2))
    (_, back_norm_inc), (query_curv, back_norm_inc_tan) = jax.jvp(
        lambda q, m, n: mem_grad(q, m, n, mem_weight),
        (query_rows, memory, normalizer),
        (query_dir, memory_tan, normalizer_tan),
    )
    norm_grads = jnp.concatenate((back_norm_inc, back_norm_inc_tan), axis=0)
    own_suffix, back_mem_tan = scan_close(backward_open, backward_layout, CTX)
    own_suffix, back_mem_tan, norm_grads = lax.optimization_barrier((own_suffix, back_mem_tan, norm_grads))
    back_mem = lax.all_gather(own_suffix, "probe", axis=0, tiled=True)

    back_norms = outer_exclusive(norm_grads, CTX, True)
    back_norm, back_norm_tan = back_norms[:heads], back_norms[heads:]

    through = jnp.einsum("shb,hab->sha", value_rows, back_mem, precision=HIGH) + back_norm[None]
    through_tan = (
        jnp.einsum("shb,hab->sha", value_dir, back_mem, precision=HIGH)
        + jnp.einsum("shb,hab->sha", value_rows, back_mem_tan, precision=HIGH)
        + back_norm_tan[None]
    )
    query_out = local_curv[0] + query_curv
    key_out = local_curv[1] + feature_curve(key_rows) * key_dir * through + key_slope * through_tan
    value_out = (
        local_curv[2]
        + jnp.einsum("sha,hab->shb", key_tan, back_mem, precision=HIGH)
        + jnp.einsum("sha,hab->shb", key_feat, back_mem_tan, precision=HIGH)
    )
    stacked = jnp.stack((query_out, key_out, value_out))
    products = stacked.reshape(1, 3, seg_rows, heads * head_size)
    partial_trace = jnp.sum(signs * stacked, axis=(1, 3)) / (seg_rows * groups)
    block_trace = lax.psum(partial_trace, "probe")
    return (products, block_trace.reshape(1, 3, heads))


def solution(mesh):
    ctx = mesh.shape["ctx"]
    inner = 4 if ctx % 4 == 0 else ctx
    devices = mesh.devices.reshape(ctx // inner, inner, mesh.shape["probe"])
    split = jax.sharding.Mesh(devices, ("outer", "inner", "probe"))
    placed = (P(None, CTX, None), P(CTX, None), P(), P("probe", None, CTX, None))
    return jax.shard_map(
        shards,
        mesh=split,
        in_specs=placed,
        out_specs=(P("probe", None, CTX, None), P(CTX, None, None)),
        check_vma=False,
    )
```

```python
import jax
import jax.numpy as jnp
from jax import lax
from jax.sharding import PartitionSpec as P

HIGH = lax.Precision.HIGH
CTX = ("outer", "inner")


def exclusive(block, reverse):
    count = block.shape[0]
    order = list(range(count - 1, -1, -1)) if reverse else list(range(count))
    sums = [None] * count
    running = jnp.zeros_like(block[0])
    for index in order:
        sums[index] = running
        running = running + block[index]
    return jnp.stack(sums)


def outer_exclusive(total, axis, reverse):
    count = lax.axis_size(axis)
    step = -1 if reverse else 1

    def shifted(value, by):
        pairs = [(i, i + step * by) for i in range(count) if 0 <= i + step * by < count]
        return lax.ppermute(value, axis, pairs)

    if count == 1:
        return jnp.zeros_like(total)
    acc = shifted(total, 1)
    by = 1
    while by < count - 1:
        acc = acc + shifted(acc, by)
        by *= 2
    return acc


def scan_open(parts, axis, reverse):
    outer, inner = axis
    count = lax.axis_size(inner)
    width = parts[0].shape[-1]
    rows = [p.reshape(-1, width) for p in parts]
    sizes = [r.shape[0] for r in rows]
    total = sum(sizes)
    unit = 8 * count
    padded = -(-total // unit) * unit
    if padded > total:
        rows.append(jnp.zeros((padded - total, width), jnp.float32))
    buffer = jnp.concatenate(rows, axis=0).reshape(count, padded // count, width)
    spread = lax.all_to_all(buffer, inner, 0, 0)
    carry = outer_exclusive(jnp.sum(spread, axis=0), outer, reverse)
    return exclusive(spread, reverse) + carry[None], (parts, sizes, padded, width)


def scan_close(scanned, layout, axis):
    parts, sizes, padded, width = layout
    back = lax.all_to_all(scanned, axis[1], 0, 0).reshape(padded, width)
    outs, row = [], 0
    for p, size in zip(parts, sizes):
        outs.append(back[row:row + size].reshape(p.shape))
        row += size
    return outs


def reduced_scan(part, axis, reverse):
    count = lax.axis_size(axis)
    place = lax.axis_index(axis)
    slot = lax.broadcasted_iota(jnp.int32, (count,) + (1,) * part.ndim, 0)
    every = lax.all_to_all(jnp.broadcast_to(part[None], (count,) + part.shape), axis, 0, 0)
    keep = (slot > place) if reverse else (slot < place)
    return jnp.sum(jnp.where(keep, every, 0.0), axis=0)


def feature_map(inputs):
    return jnp.where(inputs > 0, inputs + 1.0, jnp.exp(jnp.minimum(inputs, 0.0)))


def feature_slope(inputs):
    return jnp.where(inputs > 0, 1.0, jnp.exp(jnp.minimum(inputs, 0.0)))


def feature_curve(inputs):
    return jnp.where(inputs > 0, 0.0, jnp.exp(jnp.minimum(inputs, 0.0)))


def local_loss(query_rows, key_rows, value_rows, weight_rows):
    seg_rows = query_rows.shape[0]
    scale = query_rows.shape[-1] ** (-0.5)
    causal = lax.broadcasted_iota(jnp.int32, (seg_rows, seg_rows), 0) >= lax.broadcasted_iota(
        jnp.int32, (seg_rows, seg_rows), 1
    )
    logits = jnp.einsum("sha,tha->hst", query_rows, key_rows, precision=HIGH) * scale
    logits = jnp.where(causal[None], logits, -1e30)
    top = lax.stop_gradient(jnp.max(logits, axis=2, keepdims=True))
    weights = jnp.exp(logits - top)
    local_num = jnp.einsum("hst,thb->shb", weights, value_rows, precision=HIGH)
    local_den = jnp.transpose(jnp.sum(weights, axis=2))
    from_local = local_num / local_den[:, :, None]
    return jnp.sum(weight_rows * from_local)


def memory_loss(query_rows, memory, normalizer, weight_rows):
    query_feat = feature_map(query_rows)
    retrieved = jnp.einsum("sha,hab->shb", query_feat, memory, precision=HIGH)
    denom_mem = jnp.einsum("sha,ha->sh", query_feat, normalizer, precision=HIGH) + 1.0
    return jnp.sum(weight_rows * retrieved / denom_mem[:, :, None])


def memory_slope(query_rows, normalizer, weight_rows):
    query_feat = feature_map(query_rows)
    denom_mem = jnp.einsum("sha,ha->sh", query_feat, normalizer, precision=HIGH) + 1.0
    return jnp.einsum("sha,shb->hab", query_feat, weight_rows / denom_mem[:, :, None], precision=HIGH)


def shards(features, cotangent, gate_logits, probes):
    heads = gate_logits.shape[0]
    seg_rows = features.shape[1]
    head_size = features.shape[2] // heads
    shaped = features.reshape(3, seg_rows, heads, head_size)
    query_rows, key_rows, value_rows = (shaped[0], shaped[1], shaped[2])
    cot_rows = cotangent.reshape(seg_rows, heads, head_size)
    mixing = jax.nn.sigmoid(gate_logits)[None, :, None]
    mem_weight = cot_rows * mixing
    loc_weight = cot_rows * (1.0 - mixing)
    signs = probes[0].astype(jnp.float32).reshape(3, seg_rows, heads, head_size)
    query_dir, key_dir, value_dir = (signs[0], signs[1], signs[2])
    key_feat = feature_map(key_rows)
    key_slope = feature_slope(key_rows)
    key_tan = key_slope * key_dir
    groups = lax.axis_size("probe")
    share = heads // groups
    first_head = lax.axis_index("probe") * share

    local_grad = jax.grad(local_loss, argnums=(0, 1, 2))
    _, local_curv = jax.jvp(
        lambda q, k, v: local_grad(q, k, v, loc_weight),
        (query_rows, key_rows, value_rows),
        (query_dir, key_dir, value_dir),
    )

    increment = jnp.einsum("sha,shb->hab", key_feat, value_rows, precision=HIGH)
    increment_tan = jnp.einsum("sha,shb->hab", key_tan, value_rows, precision=HIGH) + jnp.einsum(
        "sha,shb->hab", key_feat, value_dir, precision=HIGH
    )
    norm_inc = jnp.sum(key_feat, axis=0)
    norm_tan = jnp.sum(key_tan, axis=0)
    own_inc = lax.dynamic_slice_in_dim(increment, first_head, share, 0)
    norms = reduced_scan(jnp.concatenate((norm_inc, norm_tan), axis=0), CTX, False)
    normalizer, normalizer_tan = norms[:heads], norms[heads:]
    forward_open, forward_layout = scan_open((own_inc, increment_tan), CTX, False)

    slope, slope_tan = jax.jvp(
        lambda q, n: memory_slope(q, n, mem_weight), (query_rows, normalizer), (query_dir, normalizer_tan)
    )
    own_slope = lax.dynamic_slice_in_dim(slope, first_head, share, 0)
    backward_open, backward_layout = scan_open((own_slope, slope_tan), CTX, True)
    forward_open, backward_open = lax.optimization_barrier((forward_open, backward_open))
    own_prefix, memory_tan = scan_close(forward_open, forward_layout, CTX)
    memory = lax.all_gather(own_prefix, "probe", axis=0, tiled=True)
    mem_grad = jax.grad(memory_loss, argnums=(0, 2))
    (_, back_norm_inc), (query_curv, back_norm_inc_tan) = jax.jvp(
        lambda q, m, n: mem_grad(q, m, n, mem_weight),
        (query_rows, memory, normalizer),
        (query_dir, memory_tan, normalizer_tan),
    )
    norm_grads = jnp.concatenate((back_norm_inc, back_norm_inc_tan), axis=0)
    own_suffix, back_mem_tan = scan_close(backward_open, backward_layout, CTX)
    own_suffix, back_mem_tan, norm_grads = lax.optimization_barrier((own_suffix, back_mem_tan, norm_grads))
    back_mem = lax.all_gather(own_suffix, "probe", axis=0, tiled=True)

    back_norms = reduced_scan(norm_grads, CTX, True)
    back_norm, back_norm_tan = back_norms[:heads], back_norms[heads:]

    through = jnp.einsum("shb,hab->sha", value_rows, back_mem, precision=HIGH) + back_norm[None]
    through_tan = (
        jnp.einsum("shb,hab->sha", value_dir, back_mem, precision=HIGH)
        + jnp.einsum("shb,hab->sha", value_rows, back_mem_tan, precision=HIGH)
        + back_norm_tan[None]
    )
    query_out = local_curv[0] + query_curv
    key_out = local_curv[1] + feature_curve(key_rows) * key_dir * through + key_slope * through_tan
    value_out = (
        local_curv[2]
        + jnp.einsum("sha,hab->shb", key_tan, back_mem, precision=HIGH)
        + jnp.einsum("sha,hab->shb", key_feat, back_mem_tan, precision=HIGH)
    )
    stacked = jnp.stack((query_out, key_out, value_out))
    products = stacked.reshape(1, 3, seg_rows, heads * head_size)
    partial_trace = jnp.sum(signs * stacked, axis=(1, 3)) / (seg_rows * groups)
    block_trace = lax.psum(partial_trace, "probe")
    return (products, block_trace.reshape(1, 3, heads))


def solution(mesh):
    ctx = mesh.shape["ctx"]
    inner = 4 if ctx % 4 == 0 else ctx
    devices = mesh.devices.reshape(ctx // inner, inner, mesh.shape["probe"])
    split = jax.sharding.Mesh(devices, ("outer", "inner", "probe"))
    placed = (P(None, CTX, None), P(CTX, None), P(), P("probe", None, CTX, None))
    return jax.shard_map(
        shards,
        mesh=split,
        in_specs=placed,
        out_specs=(P("probe", None, CTX, None), P(CTX, None, None)),
        check_vma=False,
    )
```

```python
import jax
import jax.numpy as jnp
from jax import lax
from jax.sharding import PartitionSpec as P

HIGH = lax.Precision.HIGH
CTX = ("outer", "inner")


def exclusive(block, reverse):
    count = block.shape[0]
    order = list(range(count - 1, -1, -1)) if reverse else list(range(count))
    sums = [None] * count
    running = jnp.zeros_like(block[0])
    for index in order:
        sums[index] = running
        running = running + block[index]
    return jnp.stack(sums)


def outer_exclusive(total, axis, reverse):
    count = lax.axis_size(axis)
    step = -1 if reverse else 1

    def shifted(value, by):
        pairs = [(i, i + step * by) for i in range(count) if 0 <= i + step * by < count]
        return lax.ppermute(value, axis, pairs)

    if count == 1:
        return jnp.zeros_like(total)
    acc = shifted(total, 1)
    by = 1
    while by < count - 1:
        acc = acc + shifted(acc, by)
        by *= 2
    return acc


def scan_open(parts, axis, reverse, tie=None):
    outer, inner = axis
    count = lax.axis_size(inner)
    width = parts[0].shape[-1]
    rows = [p.reshape(-1, width) for p in parts]
    sizes = [r.shape[0] for r in rows]
    total = sum(sizes)
    unit = 8 * count
    padded = -(-total // unit) * unit
    if padded > total:
        rows.append(jnp.zeros((padded - total, width), jnp.float32))
    buffer = jnp.concatenate(rows, axis=0).reshape(count, padded // count, width)
    spread = lax.all_to_all(buffer, inner, 0, 0)
    if tie is not None:
        spread, tie = lax.optimization_barrier((spread, tie))
    carry = outer_exclusive(jnp.sum(spread, axis=0), outer, reverse)
    return exclusive(spread, reverse) + carry[None], (parts, sizes, padded, width), tie


def scan_close(scanned, layout, axis):
    parts, sizes, padded, width = layout
    back = lax.all_to_all(scanned, axis[1], 0, 0).reshape(padded, width)
    outs, row = [], 0
    for p, size in zip(parts, sizes):
        outs.append(back[row:row + size].reshape(p.shape))
        row += size
    return outs


def reduced_scan(part, axis, reverse):
    count = lax.axis_size(axis)
    place = lax.axis_index(axis)
    slot = lax.broadcasted_iota(jnp.int32, (count,) + (1,) * part.ndim, 0)
    every = lax.all_to_all(jnp.broadcast_to(part[None], (count,) + part.shape), axis, 0, 0)
    keep = (slot > place) if reverse else (slot < place)
    return jnp.sum(jnp.where(keep, every, 0.0), axis=0)


def feature_map(inputs):
    return jnp.where(inputs > 0, inputs + 1.0, jnp.exp(jnp.minimum(inputs, 0.0)))


def feature_slope(inputs):
    return jnp.where(inputs > 0, 1.0, jnp.exp(jnp.minimum(inputs, 0.0)))


def feature_curve(inputs):
    return jnp.where(inputs > 0, 0.0, jnp.exp(jnp.minimum(inputs, 0.0)))


def local_loss(query_rows, key_rows, value_rows, weight_rows):
    seg_rows = query_rows.shape[0]
    scale = query_rows.shape[-1] ** (-0.5)
    causal = lax.broadcasted_iota(jnp.int32, (seg_rows, seg_rows), 0) >= lax.broadcasted_iota(
        jnp.int32, (seg_rows, seg_rows), 1
    )
    logits = jnp.einsum("sha,tha->hst", query_rows, key_rows, precision=HIGH) * scale
    logits = jnp.where(causal[None], logits, -1e30)
    top = lax.stop_gradient(jnp.max(logits, axis=2, keepdims=True))
    weights = jnp.exp(logits - top)
    local_num = jnp.einsum("hst,thb->shb", weights, value_rows, precision=HIGH)
    local_den = jnp.transpose(jnp.sum(weights, axis=2))
    from_local = local_num / local_den[:, :, None]
    return jnp.sum(weight_rows * from_local)


def memory_loss(query_rows, memory, normalizer, weight_rows):
    query_feat = feature_map(query_rows)
    retrieved = jnp.einsum("sha,hab->shb", query_feat, memory, precision=HIGH)
    denom_mem = jnp.einsum("sha,ha->sh", query_feat, normalizer, precision=HIGH) + 1.0
    return jnp.sum(weight_rows * retrieved / denom_mem[:, :, None])


def memory_slope(query_rows, normalizer, weight_rows):
    query_feat = feature_map(query_rows)
    denom_mem = jnp.einsum("sha,ha->sh", query_feat, normalizer, precision=HIGH) + 1.0
    return jnp.einsum("sha,shb->hab", query_feat, weight_rows / denom_mem[:, :, None], precision=HIGH)


def shards(features, cotangent, gate_logits, probes):
    heads = gate_logits.shape[0]
    seg_rows = features.shape[1]
    head_size = features.shape[2] // heads
    shaped = features.reshape(3, seg_rows, heads, head_size)
    query_rows, key_rows, value_rows = (shaped[0], shaped[1], shaped[2])
    cot_rows = cotangent.reshape(seg_rows, heads, head_size)
    mixing = jax.nn.sigmoid(gate_logits)[None, :, None]
    mem_weight = cot_rows * mixing
    loc_weight = cot_rows * (1.0 - mixing)
    signs = probes[0].astype(jnp.float32).reshape(3, seg_rows, heads, head_size)
    query_dir, key_dir, value_dir = (signs[0], signs[1], signs[2])
    key_feat = feature_map(key_rows)
    key_slope = feature_slope(key_rows)
    key_tan = key_slope * key_dir
    groups = lax.axis_size("probe")
    share = heads // groups
    first_head = lax.axis_index("probe") * share

    local_grad = jax.grad(local_loss, argnums=(0, 1, 2))
    _, local_curv = jax.jvp(
        lambda q, k, v: local_grad(q, k, v, loc_weight),
        (query_rows, key_rows, value_rows),
        (query_dir, key_dir, value_dir),
    )

    increment = jnp.einsum("sha,shb->hab", key_feat, value_rows, precision=HIGH)
    increment_tan = jnp.einsum("sha,shb->hab", key_tan, value_rows, precision=HIGH) + jnp.einsum(
        "sha,shb->hab", key_feat, value_dir, precision=HIGH
    )
    norm_inc = jnp.sum(key_feat, axis=0)
    norm_tan = jnp.sum(key_tan, axis=0)
    own_inc = lax.dynamic_slice_in_dim(increment, first_head, share, 0)
    forward_open, forward_layout, norm_rows = scan_open(
        (own_inc, increment_tan), CTX, False, jnp.concatenate((norm_inc, norm_tan), axis=0)
    )
    norms = reduced_scan(norm_rows, CTX, False)
    normalizer, normalizer_tan = norms[:heads], norms[heads:]

    slope, slope_tan = jax.jvp(
        lambda q, n: memory_slope(q, n, mem_weight), (query_rows, normalizer), (query_dir, normalizer_tan)
    )
    own_slope = lax.dynamic_slice_in_dim(slope, first_head, share, 0)
    backward_open, backward_layout, _ = scan_open((own_slope, slope_tan), CTX, True)
    forward_open, backward_open = lax.optimization_barrier((forward_open, backward_open))
    own_prefix, memory_tan = scan_close(forward_open, forward_layout, CTX)
    memory = lax.all_gather(own_prefix, "probe", axis=0, tiled=True)
    own_suffix, back_mem_tan = scan_close(backward_open, backward_layout, CTX)
    back_mem = lax.all_gather(own_suffix, "probe", axis=0, tiled=True)

    mem_grad = jax.grad(memory_loss, argnums=(0, 2))
    (_, back_norm_inc), (query_curv, back_norm_inc_tan) = jax.jvp(
        lambda q, m, n: mem_grad(q, m, n, mem_weight),
        (query_rows, memory, normalizer),
        (query_dir, memory_tan, normalizer_tan),
    )
    back_norms = reduced_scan(jnp.concatenate((back_norm_inc, back_norm_inc_tan), axis=0), CTX, True)
    back_norm, back_norm_tan = back_norms[:heads], back_norms[heads:]

    through = jnp.einsum("shb,hab->sha", value_rows, back_mem, precision=HIGH) + back_norm[None]
    through_tan = (
        jnp.einsum("shb,hab->sha", value_dir, back_mem, precision=HIGH)
        + jnp.einsum("shb,hab->sha", value_rows, back_mem_tan, precision=HIGH)
        + back_norm_tan[None]
    )
    query_out = local_curv[0] + query_curv
    key_out = local_curv[1] + feature_curve(key_rows) * key_dir * through + key_slope * through_tan
    value_out = (
        local_curv[2]
        + jnp.einsum("sha,hab->shb", key_tan, back_mem, precision=HIGH)
        + jnp.einsum("sha,hab->shb", key_feat, back_mem_tan, precision=HIGH)
    )
    stacked = jnp.stack((query_out, key_out, value_out))
    products = stacked.reshape(1, 3, seg_rows, heads * head_size)
    partial_trace = jnp.sum(signs * stacked, axis=(1, 3)) / (seg_rows * groups)
    block_trace = lax.psum(partial_trace, "probe")
    return (products, block_trace.reshape(1, 3, heads))


def solution(mesh):
    ctx = mesh.shape["ctx"]
    inner = 4 if ctx % 4 == 0 else ctx
    devices = mesh.devices.reshape(ctx // inner, inner, mesh.shape["probe"])
    split = jax.sharding.Mesh(devices, ("outer", "inner", "probe"))
    placed = (P(None, CTX, None), P(CTX, None), P(), P("probe", None, CTX, None))
    return jax.shard_map(
        shards,
        mesh=split,
        in_specs=placed,
        out_specs=(P("probe", None, CTX, None), P(CTX, None, None)),
        check_vma=False,
    )
```

```python
import jax
import jax.numpy as jnp
from jax import lax
from jax.sharding import PartitionSpec as P

HIGH = lax.Precision.HIGH
CTX = ("outer", "inner")


def exclusive(block, reverse):
    count = block.shape[0]
    order = list(range(count - 1, -1, -1)) if reverse else list(range(count))
    sums = [None] * count
    running = jnp.zeros_like(block[0])
    for index in order:
        sums[index] = running
        running = running + block[index]
    return jnp.stack(sums)


def outer_exclusive(total, axis, reverse):
    count = lax.axis_size(axis)
    step = -1 if reverse else 1

    def shifted(value, by):
        pairs = [(i, i + step * by) for i in range(count) if 0 <= i + step * by < count]
        return lax.ppermute(value, axis, pairs)

    if count == 1:
        return jnp.zeros_like(total)
    acc = shifted(total, 1)
    by = 1
    while by < count - 1:
        acc = acc + shifted(acc, by)
        by *= 2
    return acc


def scan_open(parts, axis, reverse, tie=None, cover=None, cover_args=()):
    outer, inner = axis
    count = lax.axis_size(inner)
    width = parts[0].shape[-1]
    rows = [p.reshape(-1, width) for p in parts]
    sizes = [r.shape[0] for r in rows]
    total = sum(sizes)
    unit = 8 * count
    padded = -(-total // unit) * unit
    if padded > total:
        rows.append(jnp.zeros((padded - total, width), jnp.float32))
    buffer = jnp.concatenate(rows, axis=0).reshape(count, padded // count, width)
    spread = lax.all_to_all(buffer, inner, 0, 0)
    if tie is not None:
        spread, tie = lax.optimization_barrier((spread, tie))
    total = jnp.sum(spread, axis=0)
    if cover is not None:
        total, cover_args = lax.optimization_barrier((total, cover_args))
    carry = outer_exclusive(total, outer, reverse)
    if cover is not None:
        tie = cover(*cover_args)
        carry, tie = lax.optimization_barrier((carry, tie))
    return exclusive(spread, reverse) + carry[None], (parts, sizes, padded, width), tie


def scan_close(scanned, layout, axis):
    parts, sizes, padded, width = layout
    back = lax.all_to_all(scanned, axis[1], 0, 0).reshape(padded, width)
    outs, row = [], 0
    for p, size in zip(parts, sizes):
        outs.append(back[row:row + size].reshape(p.shape))
        row += size
    return outs


def reduced_scan(part, axis, reverse):
    count = lax.axis_size(axis)
    place = lax.axis_index(axis)
    slot = lax.broadcasted_iota(jnp.int32, (count,) + (1,) * part.ndim, 0)
    every = lax.all_to_all(jnp.broadcast_to(part[None], (count,) + part.shape), axis, 0, 0)
    keep = (slot > place) if reverse else (slot < place)
    return jnp.sum(jnp.where(keep, every, 0.0), axis=0)


def feature_map(inputs):
    return jnp.where(inputs > 0, inputs + 1.0, jnp.exp(jnp.minimum(inputs, 0.0)))


def feature_slope(inputs):
    return jnp.where(inputs > 0, 1.0, jnp.exp(jnp.minimum(inputs, 0.0)))


def feature_curve(inputs):
    return jnp.where(inputs > 0, 0.0, jnp.exp(jnp.minimum(inputs, 0.0)))


def local_loss(query_rows, key_rows, value_rows, weight_rows):
    seg_rows = query_rows.shape[0]
    scale = query_rows.shape[-1] ** (-0.5)
    causal = lax.broadcasted_iota(jnp.int32, (seg_rows, seg_rows), 0) >= lax.broadcasted_iota(
        jnp.int32, (seg_rows, seg_rows), 1
    )
    logits = jnp.einsum("sha,tha->hst", query_rows, key_rows, precision=HIGH) * scale
    logits = jnp.where(causal[None], logits, -1e30)
    top = lax.stop_gradient(jnp.max(logits, axis=2, keepdims=True))
    weights = jnp.exp(logits - top)
    local_num = jnp.einsum("hst,thb->shb", weights, value_rows, precision=HIGH)
    local_den = jnp.transpose(jnp.sum(weights, axis=2))
    from_local = local_num / local_den[:, :, None]
    return jnp.sum(weight_rows * from_local)


def memory_loss(query_rows, memory, normalizer, weight_rows):
    query_feat = feature_map(query_rows)
    retrieved = jnp.einsum("sha,hab->shb", query_feat, memory, precision=HIGH)
    denom_mem = jnp.einsum("sha,ha->sh", query_feat, normalizer, precision=HIGH) + 1.0
    return jnp.sum(weight_rows * retrieved / denom_mem[:, :, None])


def memory_slope(query_rows, normalizer, weight_rows):
    query_feat = feature_map(query_rows)
    denom_mem = jnp.einsum("sha,ha->sh", query_feat, normalizer, precision=HIGH) + 1.0
    return jnp.einsum("sha,shb->hab", query_feat, weight_rows / denom_mem[:, :, None], precision=HIGH)


def shards(features, cotangent, gate_logits, probes):
    heads = gate_logits.shape[0]
    seg_rows = features.shape[1]
    head_size = features.shape[2] // heads
    shaped = features.reshape(3, seg_rows, heads, head_size)
    query_rows, key_rows, value_rows = (shaped[0], shaped[1], shaped[2])
    cot_rows = cotangent.reshape(seg_rows, heads, head_size)
    mixing = jax.nn.sigmoid(gate_logits)[None, :, None]
    mem_weight = cot_rows * mixing
    loc_weight = cot_rows * (1.0 - mixing)
    signs = probes[0].astype(jnp.float32).reshape(3, seg_rows, heads, head_size)
    query_dir, key_dir, value_dir = (signs[0], signs[1], signs[2])
    key_feat = feature_map(key_rows)
    key_slope = feature_slope(key_rows)
    key_tan = key_slope * key_dir
    groups = lax.axis_size("probe")
    share = heads // groups
    first_head = lax.axis_index("probe") * share

    local_grad = jax.grad(local_loss, argnums=(0, 1, 2))

    def local_part(q, k, v, dq, dk, dv, w):
        return jax.jvp(lambda a, b, c: local_grad(a, b, c, w), (q, k, v), (dq, dk, dv))[1]

    increment = jnp.einsum("sha,shb->hab", key_feat, value_rows, precision=HIGH)
    increment_tan = jnp.einsum("sha,shb->hab", key_tan, value_rows, precision=HIGH) + jnp.einsum(
        "sha,shb->hab", key_feat, value_dir, precision=HIGH
    )
    norm_inc = jnp.sum(key_feat, axis=0)
    norm_tan = jnp.sum(key_tan, axis=0)
    own_inc = lax.dynamic_slice_in_dim(increment, first_head, share, 0)
    forward_open, forward_layout, norm_rows = scan_open(
        (own_inc, increment_tan), CTX, False, jnp.concatenate((norm_inc, norm_tan), axis=0)
    )
    norms = reduced_scan(norm_rows, CTX, False)
    normalizer, normalizer_tan = norms[:heads], norms[heads:]

    slope, slope_tan = jax.jvp(
        lambda q, n: memory_slope(q, n, mem_weight), (query_rows, normalizer), (query_dir, normalizer_tan)
    )
    own_slope = lax.dynamic_slice_in_dim(slope, first_head, share, 0)
    backward_open, backward_layout, local_curv = scan_open(
        (own_slope, slope_tan),
        CTX,
        True,
        cover=local_part,
        cover_args=(query_rows, key_rows, value_rows, query_dir, key_dir, value_dir, loc_weight),
    )
    forward_open, backward_open = lax.optimization_barrier((forward_open, backward_open))
    own_prefix, memory_tan = scan_close(forward_open, forward_layout, CTX)
    memory = lax.all_gather(own_prefix, "probe", axis=0, tiled=True)
    own_suffix, back_mem_tan = scan_close(backward_open, backward_layout, CTX)
    back_mem = lax.all_gather(own_suffix, "probe", axis=0, tiled=True)

    mem_grad = jax.grad(memory_loss, argnums=(0, 2))
    (_, back_norm_inc), (query_curv, back_norm_inc_tan) = jax.jvp(
        lambda q, m, n: mem_grad(q, m, n, mem_weight),
        (query_rows, memory, normalizer),
        (query_dir, memory_tan, normalizer_tan),
    )
    back_norms = reduced_scan(jnp.concatenate((back_norm_inc, back_norm_inc_tan), axis=0), CTX, True)
    back_norm, back_norm_tan = back_norms[:heads], back_norms[heads:]

    through = jnp.einsum("shb,hab->sha", value_rows, back_mem, precision=HIGH) + back_norm[None]
    through_tan = (
        jnp.einsum("shb,hab->sha", value_dir, back_mem, precision=HIGH)
        + jnp.einsum("shb,hab->sha", value_rows, back_mem_tan, precision=HIGH)
        + back_norm_tan[None]
    )
    query_out = local_curv[0] + query_curv
    key_out = local_curv[1] + feature_curve(key_rows) * key_dir * through + key_slope * through_tan
    value_out = (
        local_curv[2]
        + jnp.einsum("sha,hab->shb", key_tan, back_mem, precision=HIGH)
        + jnp.einsum("sha,hab->shb", key_feat, back_mem_tan, precision=HIGH)
    )
    stacked = jnp.stack((query_out, key_out, value_out))
    products = stacked.reshape(1, 3, seg_rows, heads * head_size)
    partial_trace = jnp.sum(signs * stacked, axis=(1, 3)) / (seg_rows * groups)
    block_trace = lax.psum(partial_trace, "probe")
    return (products, block_trace.reshape(1, 3, heads))


def solution(mesh):
    ctx = mesh.shape["ctx"]
    inner = 4 if ctx % 4 == 0 else ctx
    devices = mesh.devices.reshape(ctx // inner, inner, mesh.shape["probe"])
    split = jax.sharding.Mesh(devices, ("outer", "inner", "probe"))
    placed = (P(None, CTX, None), P(CTX, None), P(), P("probe", None, CTX, None))
    return jax.shard_map(
        shards,
        mesh=split,
        in_specs=placed,
        out_specs=(P("probe", None, CTX, None), P(CTX, None, None)),
        check_vma=False,
    )
```

```python
import jax
import jax.numpy as jnp
from jax import lax
from jax.sharding import PartitionSpec as P

HIGH = lax.Precision.HIGH
CTX = ("outer", "inner")


def exclusive(block, reverse):
    count = block.shape[0]
    order = list(range(count - 1, -1, -1)) if reverse else list(range(count))
    sums = [None] * count
    running = jnp.zeros_like(block[0])
    for index in order:
        sums[index] = running
        running = running + block[index]
    return jnp.stack(sums)


def outer_exclusive(total, axis, reverse):
    count = lax.axis_size(axis)
    step = -1 if reverse else 1

    def shifted(value, by):
        pairs = [(i, i + step * by) for i in range(count) if 0 <= i + step * by < count]
        return lax.ppermute(value, axis, pairs)

    if count == 1:
        return jnp.zeros_like(total)
    acc = shifted(total, 1)
    by = 1
    while by < count - 1:
        acc = acc + shifted(acc, by)
        by *= 2
    return acc


def scan_spread(parts, axis, tie=None):
    outer, inner = axis
    count = lax.axis_size(inner)
    width = parts[0].shape[-1]
    rows = [p.reshape(-1, width) for p in parts]
    sizes = [r.shape[0] for r in rows]
    total = sum(sizes)
    unit = 8 * count
    padded = -(-total // unit) * unit
    if padded > total:
        rows.append(jnp.zeros((padded - total, width), jnp.float32))
    buffer = jnp.concatenate(rows, axis=0).reshape(count, padded // count, width)
    spread = lax.all_to_all(buffer, inner, 0, 0)
    if tie is not None:
        spread, tie = lax.optimization_barrier((spread, tie))
    return spread, (parts, sizes, padded, width), tie


def both_carries(forward_total, backward_total, outer):
    if lax.axis_size(outer) != 2:
        return outer_exclusive(forward_total, outer, False), outer_exclusive(backward_total, outer, True)
    first = lax.axis_index(outer) == 0
    sent = lax.ppermute(jnp.where(first, forward_total, backward_total), outer, [(0, 1), (1, 0)])
    return jnp.where(first, 0.0, sent), jnp.where(first, sent, 0.0)


def scan_close(scanned, layout, axis):
    parts, sizes, padded, width = layout
    back = lax.all_to_all(scanned, axis[1], 0, 0).reshape(padded, width)
    outs, row = [], 0
    for p, size in zip(parts, sizes):
        outs.append(back[row:row + size].reshape(p.shape))
        row += size
    return outs


def reduced_scan(part, axis, reverse):
    count = lax.axis_size(axis)
    place = lax.axis_index(axis)
    slot = lax.broadcasted_iota(jnp.int32, (count,) + (1,) * part.ndim, 0)
    every = lax.all_to_all(jnp.broadcast_to(part[None], (count,) + part.shape), axis, 0, 0)
    keep = (slot > place) if reverse else (slot < place)
    return jnp.sum(jnp.where(keep, every, 0.0), axis=0)


def feature_map(inputs):
    return jnp.where(inputs > 0, inputs + 1.0, jnp.exp(jnp.minimum(inputs, 0.0)))


def feature_slope(inputs):
    return jnp.where(inputs > 0, 1.0, jnp.exp(jnp.minimum(inputs, 0.0)))


def feature_curve(inputs):
    return jnp.where(inputs > 0, 0.0, jnp.exp(jnp.minimum(inputs, 0.0)))


def local_loss(query_rows, key_rows, value_rows, weight_rows):
    seg_rows = query_rows.shape[0]
    scale = query_rows.shape[-1] ** (-0.5)
    causal = lax.broadcasted_iota(jnp.int32, (seg_rows, seg_rows), 0) >= lax.broadcasted_iota(
        jnp.int32, (seg_rows, seg_rows), 1
    )
    logits = jnp.einsum("sha,tha->hst", query_rows, key_rows, precision=HIGH) * scale
    logits = jnp.where(causal[None], logits, -1e30)
    top = lax.stop_gradient(jnp.max(logits, axis=2, keepdims=True))
    weights = jnp.exp(logits - top)
    local_num = jnp.einsum("hst,thb->shb", weights, value_rows, precision=HIGH)
    local_den = jnp.transpose(jnp.sum(weights, axis=2))
    from_local = local_num / local_den[:, :, None]
    return jnp.sum(weight_rows * from_local)


def memory_loss(query_rows, memory, normalizer, weight_rows):
    query_feat = feature_map(query_rows)
    retrieved = jnp.einsum("sha,hab->shb", query_feat, memory, precision=HIGH)
    denom_mem = jnp.einsum("sha,ha->sh", query_feat, normalizer, precision=HIGH) + 1.0
    return jnp.sum(weight_rows * retrieved / denom_mem[:, :, None])


def memory_slope(query_rows, normalizer, weight_rows):
    query_feat = feature_map(query_rows)
    denom_mem = jnp.einsum("sha,ha->sh", query_feat, normalizer, precision=HIGH) + 1.0
    return jnp.einsum("sha,shb->hab", query_feat, weight_rows / denom_mem[:, :, None], precision=HIGH)


def shards(features, cotangent, gate_logits, probes):
    heads = gate_logits.shape[0]
    seg_rows = features.shape[1]
    head_size = features.shape[2] // heads
    shaped = features.reshape(3, seg_rows, heads, head_size)
    query_rows, key_rows, value_rows = (shaped[0], shaped[1], shaped[2])
    cot_rows = cotangent.reshape(seg_rows, heads, head_size)
    mixing = jax.nn.sigmoid(gate_logits)[None, :, None]
    mem_weight = cot_rows * mixing
    loc_weight = cot_rows * (1.0 - mixing)
    signs = probes[0].astype(jnp.float32).reshape(3, seg_rows, heads, head_size)
    query_dir, key_dir, value_dir = (signs[0], signs[1], signs[2])
    key_feat = feature_map(key_rows)
    key_slope = feature_slope(key_rows)
    key_tan = key_slope * key_dir
    groups = lax.axis_size("probe")
    share = heads // groups
    first_head = lax.axis_index("probe") * share

    local_grad = jax.grad(local_loss, argnums=(0, 1, 2))
    _, local_curv = jax.jvp(
        lambda q, k, v: local_grad(q, k, v, loc_weight),
        (query_rows, key_rows, value_rows),
        (query_dir, key_dir, value_dir),
    )

    increment = jnp.einsum("sha,shb->hab", key_feat, value_rows, precision=HIGH)
    increment_tan = jnp.einsum("sha,shb->hab", key_tan, value_rows, precision=HIGH) + jnp.einsum(
        "sha,shb->hab", key_feat, value_dir, precision=HIGH
    )
    norm_inc = jnp.sum(key_feat, axis=0)
    norm_tan = jnp.sum(key_tan, axis=0)
    own_inc = lax.dynamic_slice_in_dim(increment, first_head, share, 0)
    forward_spread, forward_layout, norm_rows = scan_spread(
        (own_inc, increment_tan), CTX, jnp.concatenate((norm_inc, norm_tan), axis=0)
    )
    norms = reduced_scan(norm_rows, CTX, False)
    normalizer, normalizer_tan = norms[:heads], norms[heads:]

    slope, slope_tan = jax.jvp(
        lambda q, n: memory_slope(q, n, mem_weight), (query_rows, normalizer), (query_dir, normalizer_tan)
    )
    own_slope = lax.dynamic_slice_in_dim(slope, first_head, share, 0)
    backward_spread, backward_layout, _ = scan_spread((own_slope, slope_tan), CTX)
    forward_carry, backward_carry = both_carries(
        jnp.sum(forward_spread, axis=0), jnp.sum(backward_spread, axis=0), CTX[0]
    )
    forward_open = exclusive(forward_spread, False) + forward_carry[None]
    backward_open = exclusive(backward_spread, True) + backward_carry[None]
    forward_open, backward_open = lax.optimization_barrier((forward_open, backward_open))
    own_prefix, memory_tan = scan_close(forward_open, forward_layout, CTX)
    memory = lax.all_gather(own_prefix, "probe", axis=0, tiled=True)
    own_suffix, back_mem_tan = scan_close(backward_open, backward_layout, CTX)
    back_mem = lax.all_gather(own_suffix, "probe", axis=0, tiled=True)

    mem_grad = jax.grad(memory_loss, argnums=(0, 2))
    (_, back_norm_inc), (query_curv, back_norm_inc_tan) = jax.jvp(
        lambda q, m, n: mem_grad(q, m, n, mem_weight),
        (query_rows, memory, normalizer),
        (query_dir, memory_tan, normalizer_tan),
    )
    back_norms = reduced_scan(jnp.concatenate((back_norm_inc, back_norm_inc_tan), axis=0), CTX, True)
    back_norm, back_norm_tan = back_norms[:heads], back_norms[heads:]

    through = jnp.einsum("shb,hab->sha", value_rows, back_mem, precision=HIGH) + back_norm[None]
    through_tan = (
        jnp.einsum("shb,hab->sha", value_dir, back_mem, precision=HIGH)
        + jnp.einsum("shb,hab->sha", value_rows, back_mem_tan, precision=HIGH)
        + back_norm_tan[None]
    )
    query_out = local_curv[0] + query_curv
    key_out = local_curv[1] + feature_curve(key_rows) * key_dir * through + key_slope * through_tan
    value_out = (
        local_curv[2]
        + jnp.einsum("sha,hab->shb", key_tan, back_mem, precision=HIGH)
        + jnp.einsum("sha,hab->shb", key_feat, back_mem_tan, precision=HIGH)
    )
    stacked = jnp.stack((query_out, key_out, value_out))
    products = stacked.reshape(1, 3, seg_rows, heads * head_size)
    partial_trace = jnp.sum(signs * stacked, axis=(1, 3)) / (seg_rows * groups)
    block_trace = lax.psum(partial_trace, "probe")
    return (products, block_trace.reshape(1, 3, heads))


def solution(mesh):
    ctx = mesh.shape["ctx"]
    inner = 4 if ctx % 4 == 0 else ctx
    devices = mesh.devices.reshape(ctx // inner, inner, mesh.shape["probe"])
    split = jax.sharding.Mesh(devices, ("outer", "inner", "probe"))
    placed = (P(None, CTX, None), P(CTX, None), P(), P("probe", None, CTX, None))
    return jax.shard_map(
        shards,
        mesh=split,
        in_specs=placed,
        out_specs=(P("probe", None, CTX, None), P(CTX, None, None)),
        check_vma=False,
    )
```

```python
import jax
import jax.numpy as jnp
from jax import lax
from jax.sharding import PartitionSpec as P

HIGH = lax.Precision.HIGH
CTX = ("outer", "inner")


def exclusive(block, reverse):
    count = block.shape[0]
    order = list(range(count - 1, -1, -1)) if reverse else list(range(count))
    sums = [None] * count
    running = jnp.zeros_like(block[0])
    for index in order:
        sums[index] = running
        running = running + block[index]
    return jnp.stack(sums)


def outer_exclusive(total, axis, reverse):
    count = lax.axis_size(axis)
    step = -1 if reverse else 1

    def shifted(value, by):
        pairs = [(i, i + step * by) for i in range(count) if 0 <= i + step * by < count]
        return lax.ppermute(value, axis, pairs)

    if count == 1:
        return jnp.zeros_like(total)
    acc = shifted(total, 1)
    by = 1
    while by < count - 1:
        acc = acc + shifted(acc, by)
        by *= 2
    return acc


def scan_open(parts, axis, reverse, tie=None):
    outer, inner = axis
    count = lax.axis_size(inner)
    width = parts[0].shape[-1]
    rows = [p.reshape(-1, width) for p in parts]
    sizes = [r.shape[0] for r in rows]
    total = sum(sizes)
    unit = 8 * count
    padded = -(-total // unit) * unit
    if padded > total:
        rows.append(jnp.zeros((padded - total, width), jnp.float32))
    buffer = jnp.concatenate(rows, axis=0).reshape(count, padded // count, width)
    spread = lax.all_to_all(buffer, inner, 0, 0)
    carry = outer_exclusive(jnp.sum(spread, axis=0), outer, reverse)
    if tie is not None:
        carry, tie = lax.optimization_barrier((carry, tie))
    return exclusive(spread, reverse) + carry[None], (parts, sizes, padded, width), tie


def scan_close(scanned, layout, axis):
    parts, sizes, padded, width = layout
    back = lax.all_to_all(scanned, axis[1], 0, 0).reshape(padded, width)
    outs, row = [], 0
    for p, size in zip(parts, sizes):
        outs.append(back[row:row + size].reshape(p.shape))
        row += size
    return outs


def reduced_scan(part, axis, reverse):
    count = lax.axis_size(axis)
    place = lax.axis_index(axis)
    slot = lax.broadcasted_iota(jnp.int32, (count,) + (1,) * part.ndim, 0)
    every = lax.all_to_all(jnp.broadcast_to(part[None], (count,) + part.shape), axis, 0, 0)
    keep = (slot > place) if reverse else (slot < place)
    return jnp.sum(jnp.where(keep, every, 0.0), axis=0)


def feature_map(inputs):
    return jnp.where(inputs > 0, inputs + 1.0, jnp.exp(jnp.minimum(inputs, 0.0)))


def feature_slope(inputs):
    return jnp.where(inputs > 0, 1.0, jnp.exp(jnp.minimum(inputs, 0.0)))


def feature_curve(inputs):
    return jnp.where(inputs > 0, 0.0, jnp.exp(jnp.minimum(inputs, 0.0)))


def local_loss(query_rows, key_rows, value_rows, weight_rows):
    seg_rows = query_rows.shape[0]
    scale = query_rows.shape[-1] ** (-0.5)
    causal = lax.broadcasted_iota(jnp.int32, (seg_rows, seg_rows), 0) >= lax.broadcasted_iota(
        jnp.int32, (seg_rows, seg_rows), 1
    )
    logits = jnp.einsum("sha,tha->hst", query_rows, key_rows, precision=HIGH) * scale
    logits = jnp.where(causal[None], logits, -1e30)
    top = lax.stop_gradient(jnp.max(logits, axis=2, keepdims=True))
    weights = jnp.exp(logits - top)
    local_num = jnp.einsum("hst,thb->shb", weights, value_rows, precision=HIGH)
    local_den = jnp.transpose(jnp.sum(weights, axis=2))
    from_local = local_num / local_den[:, :, None]
    return jnp.sum(weight_rows * from_local)


def memory_loss(query_rows, memory, normalizer, weight_rows):
    query_feat = feature_map(query_rows)
    retrieved = jnp.einsum("sha,hab->shb", query_feat, memory, precision=HIGH)
    denom_mem = jnp.einsum("sha,ha->sh", query_feat, normalizer, precision=HIGH) + 1.0
    return jnp.sum(weight_rows * retrieved / denom_mem[:, :, None])


def memory_slope(query_rows, normalizer, weight_rows):
    query_feat = feature_map(query_rows)
    denom_mem = jnp.einsum("sha,ha->sh", query_feat, normalizer, precision=HIGH) + 1.0
    return jnp.einsum("sha,shb->hab", query_feat, weight_rows / denom_mem[:, :, None], precision=HIGH)


def shards(features, cotangent, gate_logits, probes):
    heads = gate_logits.shape[0]
    seg_rows = features.shape[1]
    head_size = features.shape[2] // heads
    shaped = features.reshape(3, seg_rows, heads, head_size)
    query_rows, key_rows, value_rows = (shaped[0], shaped[1], shaped[2])
    cot_rows = cotangent.reshape(seg_rows, heads, head_size)
    mixing = jax.nn.sigmoid(gate_logits)[None, :, None]
    mem_weight = cot_rows * mixing
    loc_weight = cot_rows * (1.0 - mixing)
    signs = probes[0].astype(jnp.float32).reshape(3, seg_rows, heads, head_size)
    query_dir, key_dir, value_dir = (signs[0], signs[1], signs[2])
    key_feat = feature_map(key_rows)
    key_slope = feature_slope(key_rows)
    key_tan = key_slope * key_dir
    groups = lax.axis_size("probe")
    share = heads // groups
    first_head = lax.axis_index("probe") * share

    local_grad = jax.grad(local_loss, argnums=(0, 1, 2))
    _, local_curv = jax.jvp(
        lambda q, k, v: local_grad(q, k, v, loc_weight),
        (query_rows, key_rows, value_rows),
        (query_dir, key_dir, value_dir),
    )

    increment = jnp.einsum("sha,shb->hab", key_feat, value_rows, precision=HIGH)
    increment_tan = jnp.einsum("sha,shb->hab", key_tan, value_rows, precision=HIGH) + jnp.einsum(
        "sha,shb->hab", key_feat, value_dir, precision=HIGH
    )
    norm_inc = jnp.sum(key_feat, axis=0)
    norm_tan = jnp.sum(key_tan, axis=0)
    own_inc = lax.dynamic_slice_in_dim(increment, first_head, share, 0)
    forward_open, forward_layout, norm_rows = scan_open(
        (own_inc, increment_tan), CTX, False, jnp.concatenate((norm_inc, norm_tan), axis=0)
    )
    norms = reduced_scan(norm_rows, CTX, False)
    normalizer, normalizer_tan = norms[:heads], norms[heads:]

    slope, slope_tan = jax.jvp(
        lambda q, n: memory_slope(q, n, mem_weight), (query_rows, normalizer), (query_dir, normalizer_tan)
    )
    own_slope = lax.dynamic_slice_in_dim(slope, first_head, share, 0)
    backward_open, backward_layout, _ = scan_open((own_slope, slope_tan), CTX, True)
    own_prefix, memory_tan = scan_close(forward_open, forward_layout, CTX)
    memory = lax.all_gather(own_prefix, "probe", axis=0, tiled=True)
    own_suffix, back_mem_tan = scan_close(backward_open, backward_layout, CTX)
    back_mem = lax.all_gather(own_suffix, "probe", axis=0, tiled=True)

    mem_grad = jax.grad(memory_loss, argnums=(0, 2))
    (_, back_norm_inc), (query_curv, back_norm_inc_tan) = jax.jvp(
        lambda q, m, n: mem_grad(q, m, n, mem_weight),
        (query_rows, memory, normalizer),
        (query_dir, memory_tan, normalizer_tan),
    )
    back_norms = reduced_scan(jnp.concatenate((back_norm_inc, back_norm_inc_tan), axis=0), CTX, True)
    back_norm, back_norm_tan = back_norms[:heads], back_norms[heads:]

    through = jnp.einsum("shb,hab->sha", value_rows, back_mem, precision=HIGH) + back_norm[None]
    through_tan = (
        jnp.einsum("shb,hab->sha", value_dir, back_mem, precision=HIGH)
        + jnp.einsum("shb,hab->sha", value_rows, back_mem_tan, precision=HIGH)
        + back_norm_tan[None]
    )
    query_out = local_curv[0] + query_curv
    key_out = local_curv[1] + feature_curve(key_rows) * key_dir * through + key_slope * through_tan
    value_out = (
        local_curv[2]
        + jnp.einsum("sha,hab->shb", key_tan, back_mem, precision=HIGH)
        + jnp.einsum("sha,hab->shb", key_feat, back_mem_tan, precision=HIGH)
    )
    stacked = jnp.stack((query_out, key_out, value_out))
    products = stacked.reshape(1, 3, seg_rows, heads * head_size)
    partial_trace = jnp.sum(signs * stacked, axis=(1, 3)) / (seg_rows * groups)
    block_trace = lax.psum(partial_trace, "probe")
    return (products, block_trace.reshape(1, 3, heads))


def solution(mesh):
    ctx = mesh.shape["ctx"]
    inner = 4 if ctx % 4 == 0 else ctx
    devices = mesh.devices.reshape(ctx // inner, inner, mesh.shape["probe"])
    split = jax.sharding.Mesh(devices, ("outer", "inner", "probe"))
    placed = (P(None, CTX, None), P(CTX, None), P(), P("probe", None, CTX, None))
    return jax.shard_map(
        shards,
        mesh=split,
        in_specs=placed,
        out_specs=(P("probe", None, CTX, None), P(CTX, None, None)),
        check_vma=False,
    )
```

```python
import jax
import jax.numpy as jnp
from jax import lax
from jax.sharding import PartitionSpec as P

HIGH = lax.Precision.HIGH
CTX = ("outer", "inner")


def exclusive(block, reverse):
    count = block.shape[0]
    order = list(range(count - 1, -1, -1)) if reverse else list(range(count))
    sums = [None] * count
    running = jnp.zeros_like(block[0])
    for index in order:
        sums[index] = running
        running = running + block[index]
    return jnp.stack(sums)


def outer_exclusive(total, axis, reverse):
    count = lax.axis_size(axis)
    step = -1 if reverse else 1

    def shifted(value, by):
        pairs = [(i, i + step * by) for i in range(count) if 0 <= i + step * by < count]
        return lax.ppermute(value, axis, pairs)

    if count == 1:
        return jnp.zeros_like(total)
    acc = shifted(total, 1)
    by = 1
    while by < count - 1:
        acc = acc + shifted(acc, by)
        by *= 2
    return acc


def scan_open(parts, axis, reverse, tie=None):
    outer, inner = axis
    count = lax.axis_size(inner)
    width = parts[0].shape[-1]
    rows = [p.reshape(-1, width) for p in parts]
    sizes = [r.shape[0] for r in rows]
    total = sum(sizes)
    unit = 8 * count
    padded = -(-total // unit) * unit
    if padded > total:
        rows.append(jnp.zeros((padded - total, width), jnp.float32))
    buffer = jnp.concatenate(rows, axis=0).reshape(count, padded // count, width)
    spread = lax.all_to_all(buffer, inner, 0, 0)
    if tie is not None:
        spread, tie = lax.optimization_barrier((spread, tie))
    carry = outer_exclusive(jnp.sum(spread, axis=0), outer, reverse)
    return exclusive(spread, reverse) + carry[None], (parts, sizes, padded, width), tie


def scan_close(scanned, layout, axis):
    parts, sizes, padded, width = layout
    back = lax.all_to_all(scanned, axis[1], 0, 0).reshape(padded, width)
    outs, row = [], 0
    for p, size in zip(parts, sizes):
        outs.append(back[row:row + size].reshape(p.shape))
        row += size
    return outs


def reduced_scan(part, axis, reverse):
    count = lax.axis_size(axis)
    place = lax.axis_index(axis)
    slot = lax.broadcasted_iota(jnp.int32, (count,) + (1,) * part.ndim, 0)
    every = lax.all_to_all(jnp.broadcast_to(part[None], (count,) + part.shape), axis, 0, 0)
    keep = (slot > place) if reverse else (slot < place)
    return jnp.sum(jnp.where(keep, every, 0.0), axis=0)


def feature_map(inputs):
    return jnp.where(inputs > 0, inputs + 1.0, jnp.exp(jnp.minimum(inputs, 0.0)))


def feature_slope(inputs):
    return jnp.where(inputs > 0, 1.0, jnp.exp(jnp.minimum(inputs, 0.0)))


def feature_curve(inputs):
    return jnp.where(inputs > 0, 0.0, jnp.exp(jnp.minimum(inputs, 0.0)))


def local_loss(query_rows, key_rows, value_rows, weight_rows):
    seg_rows = query_rows.shape[0]
    scale = query_rows.shape[-1] ** (-0.5)
    causal = lax.broadcasted_iota(jnp.int32, (seg_rows, seg_rows), 0) >= lax.broadcasted_iota(
        jnp.int32, (seg_rows, seg_rows), 1
    )
    logits = jnp.einsum("sha,tha->hst", query_rows, key_rows, precision=HIGH) * scale
    logits = jnp.where(causal[None], logits, -1e30)
    top = lax.stop_gradient(jnp.max(logits, axis=2, keepdims=True))
    weights = jnp.exp(logits - top)
    local_num = jnp.einsum("hst,thb->shb", weights, value_rows, precision=HIGH)
    local_den = jnp.transpose(jnp.sum(weights, axis=2))
    from_local = local_num / local_den[:, :, None]
    return jnp.sum(weight_rows * from_local)


def memory_loss(query_rows, memory, normalizer, weight_rows):
    query_feat = feature_map(query_rows)
    retrieved = jnp.einsum("sha,hab->shb", query_feat, memory, precision=HIGH)
    denom_mem = jnp.einsum("sha,ha->sh", query_feat, normalizer, precision=HIGH) + 1.0
    return jnp.sum(weight_rows * retrieved / denom_mem[:, :, None])


def memory_slope(query_rows, normalizer, weight_rows):
    query_feat = feature_map(query_rows)
    denom_mem = jnp.einsum("sha,ha->sh", query_feat, normalizer, precision=HIGH) + 1.0
    return jnp.einsum("sha,shb->hab", query_feat, weight_rows / denom_mem[:, :, None], precision=HIGH)


def shards(features, cotangent, gate_logits, probes):
    heads = gate_logits.shape[0]
    seg_rows = features.shape[1]
    head_size = features.shape[2] // heads
    shaped = features.reshape(3, seg_rows, heads, head_size)
    query_rows, key_rows, value_rows = (shaped[0], shaped[1], shaped[2])
    cot_rows = cotangent.reshape(seg_rows, heads, head_size)
    mixing = jax.nn.sigmoid(gate_logits)[None, :, None]
    mem_weight = cot_rows * mixing
    loc_weight = cot_rows * (1.0 - mixing)
    signs = probes[0].astype(jnp.float32).reshape(3, seg_rows, heads, head_size)
    query_dir, key_dir, value_dir = (signs[0], signs[1], signs[2])
    key_feat = feature_map(key_rows)
    key_slope = feature_slope(key_rows)
    key_tan = key_slope * key_dir
    groups = lax.axis_size("probe")
    share = heads // groups
    first_head = lax.axis_index("probe") * share

    local_grad = jax.grad(local_loss, argnums=(0, 1, 2))
    _, local_curv = jax.jvp(
        lambda q, k, v: local_grad(q, k, v, loc_weight),
        (query_rows, key_rows, value_rows),
        (query_dir, key_dir, value_dir),
    )

    increment = jnp.einsum("sha,shb->hab", key_feat, value_rows, precision=HIGH)
    increment_tan = jnp.einsum("sha,shb->hab", key_tan, value_rows, precision=HIGH) + jnp.einsum(
        "sha,shb->hab", key_feat, value_dir, precision=HIGH
    )
    norm_inc = jnp.sum(key_feat, axis=0)
    norm_tan = jnp.sum(key_tan, axis=0)
    own_inc = lax.dynamic_slice_in_dim(increment, first_head, share, 0)
    forward_open, forward_layout, norm_rows = scan_open(
        (own_inc, increment_tan), CTX, False, jnp.concatenate((norm_inc, norm_tan), axis=0)
    )
    norms = reduced_scan(norm_rows, CTX, False)
    normalizer, normalizer_tan = norms[:heads], norms[heads:]

    slope, slope_tan = jax.jvp(
        lambda q, n: memory_slope(q, n, mem_weight), (query_rows, normalizer), (query_dir, normalizer_tan)
    )
    own_slope = lax.dynamic_slice_in_dim(slope, first_head, share, 0)
    backward_open, backward_layout, _ = scan_open((own_slope, slope_tan), CTX, True)
    forward_open, backward_open = lax.optimization_barrier((forward_open, backward_open))
    own_prefix, memory_tan = scan_close(forward_open, forward_layout, CTX)
    memory = lax.all_gather(own_prefix, "probe", axis=0, tiled=True)
    own_suffix, back_mem_tan = scan_close(backward_open, backward_layout, CTX)
    back_mem = lax.all_gather(own_suffix, "probe", axis=0, tiled=True)

    mem_grad = jax.grad(memory_loss, argnums=(0, 2))
    (_, back_norm_inc), (query_curv, back_norm_inc_tan) = jax.jvp(
        lambda q, m, n: mem_grad(q, m, n, mem_weight),
        (query_rows, memory, normalizer),
        (query_dir, memory_tan, normalizer_tan),
    )
    back_norms = reduced_scan(jnp.concatenate((back_norm_inc, back_norm_inc_tan), axis=0), CTX, True)
    back_norm, back_norm_tan = back_norms[:heads], back_norms[heads:]

    through = jnp.einsum("shb,hab->sha", value_rows, back_mem, precision=HIGH) + back_norm[None]
    through_tan = (
        jnp.einsum("shb,hab->sha", value_dir, back_mem, precision=HIGH)
        + jnp.einsum("shb,hab->sha", value_rows, back_mem_tan, precision=HIGH)
        + back_norm_tan[None]
    )
    query_out = local_curv[0] + query_curv
    key_out = local_curv[1] + feature_curve(key_rows) * key_dir * through + key_slope * through_tan
    value_out = (
        local_curv[2]
        + jnp.einsum("sha,hab->shb", key_tan, back_mem, precision=HIGH)
        + jnp.einsum("sha,hab->shb", key_feat, back_mem_tan, precision=HIGH)
    )
    stacked = jnp.stack((query_out, key_out, value_out))
    products = stacked.reshape(1, 3, seg_rows, heads * head_size)
    partial_trace = jnp.sum(signs * stacked, axis=(1, 3)) / (seg_rows * groups)
    block_trace = jnp.sum(
        lax.all_to_all(jnp.broadcast_to(partial_trace[None], (groups,) + partial_trace.shape), "probe", 0, 0), axis=0
    )
    return (products, block_trace.reshape(1, 3, heads))


def solution(mesh):
    ctx = mesh.shape["ctx"]
    inner = 4 if ctx % 4 == 0 else ctx
    devices = mesh.devices.reshape(ctx // inner, inner, mesh.shape["probe"])
    split = jax.sharding.Mesh(devices, ("outer", "inner", "probe"))
    placed = (P(None, CTX, None), P(CTX, None), P(), P("probe", None, CTX, None))
    return jax.shard_map(
        shards,
        mesh=split,
        in_specs=placed,
        out_specs=(P("probe", None, CTX, None), P(CTX, None, None)),
        check_vma=False,
    )
```

```python
import jax
import jax.numpy as jnp
from jax import lax
from jax.sharding import PartitionSpec as P

HIGH = lax.Precision.HIGH
CTX = ("outer", "inner")


def exclusive(block, reverse):
    count = block.shape[0]
    order = list(range(count - 1, -1, -1)) if reverse else list(range(count))
    sums = [None] * count
    running = jnp.zeros_like(block[0])
    for index in order:
        sums[index] = running
        running = running + block[index]
    return jnp.stack(sums)


def outer_exclusive(total, axis, reverse):
    count = lax.axis_size(axis)
    step = -1 if reverse else 1

    def shifted(value, by):
        pairs = [(i, i + step * by) for i in range(count) if 0 <= i + step * by < count]
        return lax.ppermute(value, axis, pairs)

    if count == 1:
        return jnp.zeros_like(total)
    acc = shifted(total, 1)
    by = 1
    while by < count - 1:
        acc = acc + shifted(acc, by)
        by *= 2
    return acc


def scan_open(parts, axis, reverse, tie=None):
    outer, inner = axis
    count = lax.axis_size(inner)
    width = parts[0].shape[-1]
    rows = [p.reshape(-1, width) for p in parts]
    sizes = [r.shape[0] for r in rows]
    total = sum(sizes)
    unit = 8 * count
    padded = -(-total // unit) * unit
    if padded > total:
        rows.append(jnp.zeros((padded - total, width), jnp.float32))
    buffer = jnp.concatenate(rows, axis=0).reshape(count, padded // count, width)
    if tie is not None:
        buffer = jnp.concatenate((buffer, jnp.broadcast_to(tie[None], (count,) + tie.shape)), axis=1)
    spread = lax.all_to_all(buffer, inner, 0, 0)
    if tie is not None:
        spread, riders = spread[:, : padded // count], spread[:, padded // count :]
        member = lax.axis_index(inner)
        slot = lax.broadcasted_iota(jnp.int32, (count, 1, 1), 0)
        keep = (slot > member) if reverse else (slot < member)
        within = jnp.sum(jnp.where(keep, riders, 0.0), axis=0)
        tie = within + outer_exclusive(jnp.sum(riders, axis=0), outer, reverse)
    carry = outer_exclusive(jnp.sum(spread, axis=0), outer, reverse)
    return exclusive(spread, reverse) + carry[None], (parts, sizes, padded, width), tie


def scan_close(scanned, layout, axis):
    parts, sizes, padded, width = layout
    back = lax.all_to_all(scanned, axis[1], 0, 0).reshape(padded, width)
    outs, row = [], 0
    for p, size in zip(parts, sizes):
        outs.append(back[row:row + size].reshape(p.shape))
        row += size
    return outs


def reduced_scan(part, axis, reverse):
    count = lax.axis_size(axis)
    place = lax.axis_index(axis)
    slot = lax.broadcasted_iota(jnp.int32, (count,) + (1,) * part.ndim, 0)
    every = lax.all_to_all(jnp.broadcast_to(part[None], (count,) + part.shape), axis, 0, 0)
    keep = (slot > place) if reverse else (slot < place)
    return jnp.sum(jnp.where(keep, every, 0.0), axis=0)


def feature_map(inputs):
    return jnp.where(inputs > 0, inputs + 1.0, jnp.exp(jnp.minimum(inputs, 0.0)))


def feature_slope(inputs):
    return jnp.where(inputs > 0, 1.0, jnp.exp(jnp.minimum(inputs, 0.0)))


def feature_curve(inputs):
    return jnp.where(inputs > 0, 0.0, jnp.exp(jnp.minimum(inputs, 0.0)))


def local_loss(query_rows, key_rows, value_rows, weight_rows):
    seg_rows = query_rows.shape[0]
    scale = query_rows.shape[-1] ** (-0.5)
    causal = lax.broadcasted_iota(jnp.int32, (seg_rows, seg_rows), 0) >= lax.broadcasted_iota(
        jnp.int32, (seg_rows, seg_rows), 1
    )
    logits = jnp.einsum("sha,tha->hst", query_rows, key_rows, precision=HIGH) * scale
    logits = jnp.where(causal[None], logits, -1e30)
    top = lax.stop_gradient(jnp.max(logits, axis=2, keepdims=True))
    weights = jnp.exp(logits - top)
    local_num = jnp.einsum("hst,thb->shb", weights, value_rows, precision=HIGH)
    local_den = jnp.transpose(jnp.sum(weights, axis=2))
    from_local = local_num / local_den[:, :, None]
    return jnp.sum(weight_rows * from_local)


def memory_loss(query_rows, memory, normalizer, weight_rows):
    query_feat = feature_map(query_rows)
    retrieved = jnp.einsum("sha,hab->shb", query_feat, memory, precision=HIGH)
    denom_mem = jnp.einsum("sha,ha->sh", query_feat, normalizer, precision=HIGH) + 1.0
    return jnp.sum(weight_rows * retrieved / denom_mem[:, :, None])


def memory_slope(query_rows, normalizer, weight_rows):
    query_feat = feature_map(query_rows)
    denom_mem = jnp.einsum("sha,ha->sh", query_feat, normalizer, precision=HIGH) + 1.0
    return jnp.einsum("sha,shb->hab", query_feat, weight_rows / denom_mem[:, :, None], precision=HIGH)


def shards(features, cotangent, gate_logits, probes):
    heads = gate_logits.shape[0]
    seg_rows = features.shape[1]
    head_size = features.shape[2] // heads
    shaped = features.reshape(3, seg_rows, heads, head_size)
    query_rows, key_rows, value_rows = (shaped[0], shaped[1], shaped[2])
    cot_rows = cotangent.reshape(seg_rows, heads, head_size)
    mixing = jax.nn.sigmoid(gate_logits)[None, :, None]
    mem_weight = cot_rows * mixing
    loc_weight = cot_rows * (1.0 - mixing)
    signs = probes[0].astype(jnp.float32).reshape(3, seg_rows, heads, head_size)
    query_dir, key_dir, value_dir = (signs[0], signs[1], signs[2])
    key_feat = feature_map(key_rows)
    key_slope = feature_slope(key_rows)
    key_tan = key_slope * key_dir
    groups = lax.axis_size("probe")
    share = heads // groups
    first_head = lax.axis_index("probe") * share

    local_grad = jax.grad(local_loss, argnums=(0, 1, 2))
    _, local_curv = jax.jvp(
        lambda q, k, v: local_grad(q, k, v, loc_weight),
        (query_rows, key_rows, value_rows),
        (query_dir, key_dir, value_dir),
    )

    increment = jnp.einsum("sha,shb->hab", key_feat, value_rows, precision=HIGH)
    increment_tan = jnp.einsum("sha,shb->hab", key_tan, value_rows, precision=HIGH) + jnp.einsum(
        "sha,shb->hab", key_feat, value_dir, precision=HIGH
    )
    norm_inc = jnp.sum(key_feat, axis=0)
    norm_tan = jnp.sum(key_tan, axis=0)
    own_inc = lax.dynamic_slice_in_dim(increment, first_head, share, 0)
    forward_open, forward_layout, norm_rows = scan_open(
        (own_inc, increment_tan), CTX, False, jnp.concatenate((norm_inc, norm_tan), axis=0)
    )
    norms = norm_rows
    normalizer, normalizer_tan = norms[:heads], norms[heads:]

    slope, slope_tan = jax.jvp(
        lambda q, n: memory_slope(q, n, mem_weight), (query_rows, normalizer), (query_dir, normalizer_tan)
    )
    own_slope = lax.dynamic_slice_in_dim(slope, first_head, share, 0)
    backward_open, backward_layout, _ = scan_open((own_slope, slope_tan), CTX, True)
    forward_open, backward_open = lax.optimization_barrier((forward_open, backward_open))
    own_prefix, memory_tan = scan_close(forward_open, forward_layout, CTX)
    memory = lax.all_gather(own_prefix, "probe", axis=0, tiled=True)
    own_suffix, back_mem_tan = scan_close(backward_open, backward_layout, CTX)
    back_mem = lax.all_gather(own_suffix, "probe", axis=0, tiled=True)

    mem_grad = jax.grad(memory_loss, argnums=(0, 2))
    (_, back_norm_inc), (query_curv, back_norm_inc_tan) = jax.jvp(
        lambda q, m, n: mem_grad(q, m, n, mem_weight),
        (query_rows, memory, normalizer),
        (query_dir, memory_tan, normalizer_tan),
    )
    back_norms = reduced_scan(jnp.concatenate((back_norm_inc, back_norm_inc_tan), axis=0), CTX, True)
    back_norm, back_norm_tan = back_norms[:heads], back_norms[heads:]

    through = jnp.einsum("shb,hab->sha", value_rows, back_mem, precision=HIGH) + back_norm[None]
    through_tan = (
        jnp.einsum("shb,hab->sha", value_dir, back_mem, precision=HIGH)
        + jnp.einsum("shb,hab->sha", value_rows, back_mem_tan, precision=HIGH)
        + back_norm_tan[None]
    )
    query_out = local_curv[0] + query_curv
    key_out = local_curv[1] + feature_curve(key_rows) * key_dir * through + key_slope * through_tan
    value_out = (
        local_curv[2]
        + jnp.einsum("sha,hab->shb", key_tan, back_mem, precision=HIGH)
        + jnp.einsum("sha,hab->shb", key_feat, back_mem_tan, precision=HIGH)
    )
    stacked = jnp.stack((query_out, key_out, value_out))
    products = stacked.reshape(1, 3, seg_rows, heads * head_size)
    partial_trace = jnp.sum(signs * stacked, axis=(1, 3)) / (seg_rows * groups)
    block_trace = lax.psum(partial_trace, "probe")
    return (products, block_trace.reshape(1, 3, heads))


def solution(mesh):
    ctx = mesh.shape["ctx"]
    inner = 4 if ctx % 4 == 0 else ctx
    devices = mesh.devices.reshape(ctx // inner, inner, mesh.shape["probe"])
    split = jax.sharding.Mesh(devices, ("outer", "inner", "probe"))
    placed = (P(None, CTX, None), P(CTX, None), P(), P("probe", None, CTX, None))
    return jax.shard_map(
        shards,
        mesh=split,
        in_specs=placed,
        out_specs=(P("probe", None, CTX, None), P(CTX, None, None)),
        check_vma=False,
    )
```

```python
import jax
import jax.numpy as jnp
from jax import lax
from jax.sharding import PartitionSpec as P

HIGH = lax.Precision.HIGH
CTX = ("outer", "inner")


def exclusive(block, reverse):
    count = block.shape[0]
    order = list(range(count - 1, -1, -1)) if reverse else list(range(count))
    sums = [None] * count
    running = jnp.zeros_like(block[0])
    for index in order:
        sums[index] = running
        running = running + block[index]
    return jnp.stack(sums)


def outer_exclusive(total, axis, reverse):
    count = lax.axis_size(axis)
    step = -1 if reverse else 1

    def shifted(value, by):
        pairs = [(i, i + step * by) for i in range(count) if 0 <= i + step * by < count]
        return lax.ppermute(value, axis, pairs)

    if count == 1:
        return jnp.zeros_like(total)
    acc = shifted(total, 1)
    by = 1
    while by < count - 1:
        acc = acc + shifted(acc, by)
        by *= 2
    return acc


def scan_open(parts, axis, reverse, tie=None):
    outer, inner = axis
    count = lax.axis_size(inner)
    width = parts[0].shape[-1]
    rows = [p.reshape(-1, width) for p in parts]
    sizes = [r.shape[0] for r in rows]
    total = sum(sizes)
    unit = 8 * count
    padded = -(-total // unit) * unit
    if padded > total:
        rows.append(jnp.zeros((padded - total, width), jnp.float32))
    buffer = jnp.concatenate(rows, axis=0).reshape(count, padded // count, width)
    if tie is not None:
        buffer = jnp.concatenate((buffer, jnp.broadcast_to(tie[None], (count,) + tie.shape)), axis=1)
    spread = lax.all_to_all(buffer, inner, 0, 0)
    if tie is not None:
        spread, riders = spread[:, : padded // count], spread[:, padded // count :]
        member = lax.axis_index(inner)
        slot = lax.broadcasted_iota(jnp.int32, (count, 1, 1), 0)
        keep = (slot > member) if reverse else (slot < member)
        within = jnp.sum(jnp.where(keep, riders, 0.0), axis=0)
        both = outer_exclusive(
            jnp.concatenate((jnp.sum(spread, axis=0), jnp.sum(riders, axis=0)), axis=0), outer, reverse
        )
        carry, tie = both[: padded // count], within + both[padded // count :]
    else:
        carry = outer_exclusive(jnp.sum(spread, axis=0), outer, reverse)
    return exclusive(spread, reverse) + carry[None], (parts, sizes, padded, width), tie


def scan_close(scanned, layout, axis):
    parts, sizes, padded, width = layout
    back = lax.all_to_all(scanned, axis[1], 0, 0).reshape(padded, width)
    outs, row = [], 0
    for p, size in zip(parts, sizes):
        outs.append(back[row:row + size].reshape(p.shape))
        row += size
    return outs


def reduced_scan(part, axis, reverse):
    count = lax.axis_size(axis)
    place = lax.axis_index(axis)
    slot = lax.broadcasted_iota(jnp.int32, (count,) + (1,) * part.ndim, 0)
    every = lax.all_to_all(jnp.broadcast_to(part[None], (count,) + part.shape), axis, 0, 0)
    keep = (slot > place) if reverse else (slot < place)
    return jnp.sum(jnp.where(keep, every, 0.0), axis=0)


def feature_map(inputs):
    return jnp.where(inputs > 0, inputs + 1.0, jnp.exp(jnp.minimum(inputs, 0.0)))


def feature_slope(inputs):
    return jnp.where(inputs > 0, 1.0, jnp.exp(jnp.minimum(inputs, 0.0)))


def feature_curve(inputs):
    return jnp.where(inputs > 0, 0.0, jnp.exp(jnp.minimum(inputs, 0.0)))


def local_loss(query_rows, key_rows, value_rows, weight_rows):
    seg_rows = query_rows.shape[0]
    scale = query_rows.shape[-1] ** (-0.5)
    causal = lax.broadcasted_iota(jnp.int32, (seg_rows, seg_rows), 0) >= lax.broadcasted_iota(
        jnp.int32, (seg_rows, seg_rows), 1
    )
    logits = jnp.einsum("sha,tha->hst", query_rows, key_rows, precision=HIGH) * scale
    logits = jnp.where(causal[None], logits, -1e30)
    top = lax.stop_gradient(jnp.max(logits, axis=2, keepdims=True))
    weights = jnp.exp(logits - top)
    local_num = jnp.einsum("hst,thb->shb", weights, value_rows, precision=HIGH)
    local_den = jnp.transpose(jnp.sum(weights, axis=2))
    from_local = local_num / local_den[:, :, None]
    return jnp.sum(weight_rows * from_local)


def memory_loss(query_rows, memory, normalizer, weight_rows):
    query_feat = feature_map(query_rows)
    retrieved = jnp.einsum("sha,hab->shb", query_feat, memory, precision=HIGH)
    denom_mem = jnp.einsum("sha,ha->sh", query_feat, normalizer, precision=HIGH) + 1.0
    return jnp.sum(weight_rows * retrieved / denom_mem[:, :, None])


def memory_slope(query_rows, normalizer, weight_rows):
    query_feat = feature_map(query_rows)
    denom_mem = jnp.einsum("sha,ha->sh", query_feat, normalizer, precision=HIGH) + 1.0
    return jnp.einsum("sha,shb->hab", query_feat, weight_rows / denom_mem[:, :, None], precision=HIGH)


def shards(features, cotangent, gate_logits, probes):
    heads = gate_logits.shape[0]
    seg_rows = features.shape[1]
    head_size = features.shape[2] // heads
    shaped = features.reshape(3, seg_rows, heads, head_size)
    query_rows, key_rows, value_rows = (shaped[0], shaped[1], shaped[2])
    cot_rows = cotangent.reshape(seg_rows, heads, head_size)
    mixing = jax.nn.sigmoid(gate_logits)[None, :, None]
    mem_weight = cot_rows * mixing
    loc_weight = cot_rows * (1.0 - mixing)
    signs = probes[0].astype(jnp.float32).reshape(3, seg_rows, heads, head_size)
    query_dir, key_dir, value_dir = (signs[0], signs[1], signs[2])
    key_feat = feature_map(key_rows)
    key_slope = feature_slope(key_rows)
    key_tan = key_slope * key_dir
    groups = lax.axis_size("probe")
    share = heads // groups
    first_head = lax.axis_index("probe") * share

    local_grad = jax.grad(local_loss, argnums=(0, 1, 2))
    _, local_curv = jax.jvp(
        lambda q, k, v: local_grad(q, k, v, loc_weight),
        (query_rows, key_rows, value_rows),
        (query_dir, key_dir, value_dir),
    )

    increment = jnp.einsum("sha,shb->hab", key_feat, value_rows, precision=HIGH)
    increment_tan = jnp.einsum("sha,shb->hab", key_tan, value_rows, precision=HIGH) + jnp.einsum(
        "sha,shb->hab", key_feat, value_dir, precision=HIGH
    )
    norm_inc = jnp.sum(key_feat, axis=0)
    norm_tan = jnp.sum(key_tan, axis=0)
    own_inc = lax.dynamic_slice_in_dim(increment, first_head, share, 0)
    forward_open, forward_layout, norm_rows = scan_open(
        (own_inc, increment_tan), CTX, False, jnp.concatenate((norm_inc, norm_tan), axis=0)
    )
    norms = norm_rows
    normalizer, normalizer_tan = norms[:heads], norms[heads:]

    slope, slope_tan = jax.jvp(
        lambda q, n: memory_slope(q, n, mem_weight), (query_rows, normalizer), (query_dir, normalizer_tan)
    )
    own_slope = lax.dynamic_slice_in_dim(slope, first_head, share, 0)
    backward_open, backward_layout, _ = scan_open((own_slope, slope_tan), CTX, True)
    forward_open, backward_open = lax.optimization_barrier((forward_open, backward_open))
    own_prefix, memory_tan = scan_close(forward_open, forward_layout, CTX)
    memory = lax.all_gather(own_prefix, "probe", axis=0, tiled=True)
    own_suffix, back_mem_tan = scan_close(backward_open, backward_layout, CTX)
    back_mem = lax.all_gather(own_suffix, "probe", axis=0, tiled=True)

    mem_grad = jax.grad(memory_loss, argnums=(0, 2))
    (_, back_norm_inc), (query_curv, back_norm_inc_tan) = jax.jvp(
        lambda q, m, n: mem_grad(q, m, n, mem_weight),
        (query_rows, memory, normalizer),
        (query_dir, memory_tan, normalizer_tan),
    )
    back_norms = reduced_scan(jnp.concatenate((back_norm_inc, back_norm_inc_tan), axis=0), CTX, True)
    back_norm, back_norm_tan = back_norms[:heads], back_norms[heads:]

    through = jnp.einsum("shb,hab->sha", value_rows, back_mem, precision=HIGH) + back_norm[None]
    through_tan = (
        jnp.einsum("shb,hab->sha", value_dir, back_mem, precision=HIGH)
        + jnp.einsum("shb,hab->sha", value_rows, back_mem_tan, precision=HIGH)
        + back_norm_tan[None]
    )
    query_out = local_curv[0] + query_curv
    key_out = local_curv[1] + feature_curve(key_rows) * key_dir * through + key_slope * through_tan
    value_out = (
        local_curv[2]
        + jnp.einsum("sha,hab->shb", key_tan, back_mem, precision=HIGH)
        + jnp.einsum("sha,hab->shb", key_feat, back_mem_tan, precision=HIGH)
    )
    stacked = jnp.stack((query_out, key_out, value_out))
    products = stacked.reshape(1, 3, seg_rows, heads * head_size)
    partial_trace = jnp.sum(signs * stacked, axis=(1, 3)) / (seg_rows * groups)
    block_trace = lax.psum(partial_trace, "probe")
    return (products, block_trace.reshape(1, 3, heads))


def solution(mesh):
    ctx = mesh.shape["ctx"]
    inner = 4 if ctx % 4 == 0 else ctx
    devices = mesh.devices.reshape(ctx // inner, inner, mesh.shape["probe"])
    split = jax.sharding.Mesh(devices, ("outer", "inner", "probe"))
    placed = (P(None, CTX, None), P(CTX, None), P(), P("probe", None, CTX, None))
    return jax.shard_map(
        shards,
        mesh=split,
        in_specs=placed,
        out_specs=(P("probe", None, CTX, None), P(CTX, None, None)),
        check_vma=False,
    )
```
